32 devices in a mesh: head: 2 (over x), seq: 16 (over z, y, core).
Axes of the slice: x: 2, y: 2, z: 4, core: 2. Of those that a mesh axis runs over, the one named last changes fastest.
Arguments:
- queries: bfloat16 [4096, 5120], P('seq', 'head'), may hold values from -6 to 6
- keys: bfloat16 [4096, 5120], P('seq', 'head'), may hold values from -6 to 6
- values: bfloat16 [4096, 5120], P('seq', 'head'), may hold values from -6 to 6
- out_weight: bfloat16 [5120, 5120], P('head', 'seq'), may hold values from -0.3125 to 0.3125
- tile_lists: int32 [32, 12], replicated, may hold values from 0 to 31, as said below
- tile_counts: int32 [32], replicated, may hold values from 1 to 12, as said below
Outputs:
- mixed: bfloat16 [4096, 5120], P('seq', 'head')
The draws below stay inside these ranges and needn't reach their ends.
Inputs may be any that keep to these rules, and one draw needn't show every extreme that they name: `tile_lists`: each row q holds 12 distinct key tiles; its first entry is q itself; every entry k has |k div 2 - q div 2| <= 5. Entries after the first tile_counts[q] take no part. `tile_counts`: some query tile uses all 12 entries of its list.
All inputs are finite; a program needn't handle non-finite values.
Results may differ from the reference program's by a relative error of at most 0.008.
Values may be sent and summed in bfloat16 or wider, within the bound.
No kernel may reach another device: no remote copies, remote signals or barrier semaphores. Data moves between devices by JAX's collectives and lax.ppermute only.
A program may use at most 192 MiB of HBM per device.

```python
import math
import jax
import jax.numpy as jnp
from jax import lax

D = 5120
HEADS = 40
HD = 128
TILE = 128
TILES_DEV = 2
REACH = 5
GROUPS = 2
NT = 32
TOKENS = 4096
KMAX = 12


def normal_field(key):
    return jnp.clip(1.4 * jax.random.normal(key, (TOKENS, HEADS * HD), jnp.float32), -6.0, 6.0)


def draw_queries(key, part):
    base_field = normal_field(jax.random.fold_in(key, 1))
    return base_field.astype(jnp.bfloat16)


def draw_keys(key, part):
    base_field = normal_field(jax.random.fold_in(key, 2))
    return base_field.astype(jnp.bfloat16)


def tile_layout(key):
    slot_count = (2 * REACH + 1) * TILES_DEV
    query_ids = jnp.arange(NT, dtype=jnp.int32)
    candidates = (query_ids[:, None] // TILES_DEV - REACH) * TILES_DEV + jnp.arange(slot_count, dtype=jnp.int32)[None, :]
    inside = (candidates >= 0) & (candidates < NT)
    ranking = jax.random.randint(key, (NT, slot_count), 0, 1 << 20)
    ranking = jnp.where(inside, ranking, 1 << 21)
    ranking = jnp.where(candidates == query_ids[:, None], -1, ranking)
    ordering = jnp.argsort(ranking, axis=1, stable=True)[:, :KMAX]
    return jnp.take_along_axis(candidates, ordering, axis=1).astype(jnp.int32)


def draw_tile_lists(key, part):
    return tile_layout(jax.random.fold_in(key, 21))


def draw_tile_counts(key, part):
    drawn_counts = jax.random.randint(jax.random.fold_in(key, 31), (NT,), 1, KMAX + 1)
    picked = jax.random.randint(jax.random.fold_in(key, 32), (), 0, NT)
    return jnp.where(jnp.arange(NT, dtype=jnp.int32) == picked, KMAX, drawn_counts).astype(jnp.int32)


def shard_levels(stream_key, dims, cuts, smallest, largest):
    loudness, own = 1.0, jax.random.fold_in(stream_key, 6)
    for axis_at, parts in cuts:
        steps = jnp.exp(jax.random.uniform(jax.random.fold_in(own, axis_at), (parts,), jnp.float32, smallest / len(cuts), largest / len(cuts)))
        loudness = loudness * jnp.repeat(steps, dims[axis_at] // parts).reshape([-1 if axis == axis_at else 1 for axis in range(len(dims))])
    return loudness


def scatter_about(own_key, shape, spread, bound, cuts=(), kind=jnp.bfloat16):
    drawn = jax.random.normal(own_key, shape, jnp.float32) * spread
    if len(cuts) > 0:
        drawn = shard_levels(own_key, shape, cuts, -0.22, 0.18) * drawn
    return jnp.clip(drawn, min=-bound, max=bound).astype(kind)


def setup_inputs(seed: int = 0) -> dict:
    streams_of = jax.random.split(jax.random.key(seed), 7)
    queries = draw_queries(jax.random.fold_in(streams_of[6], 71), 0)
    keys = draw_keys(jax.random.fold_in(streams_of[6], 71), 0)
    values = scatter_about(streams_of[2], (TOKENS, HEADS * HD), 1.0, 6.0, ((0, 16), (1, 2)))
    out_weight = scatter_about(streams_of[3], (HEADS * HD, D), (HEADS * HD // 16) ** -0.5, 0.3125, ((0, 2), (1, 16)))
    tile_lists = draw_tile_lists(jax.random.fold_in(streams_of[6], 71), 0)
    tile_counts = draw_tile_counts(jax.random.fold_in(streams_of[6], 71), 0)
    return {"queries": queries, "keys": keys, "values": values, "out_weight": out_weight, "tile_lists": tile_lists, "tile_counts": tile_counts}


masked_floor = -1e+30

def tile_attention(tile_index, query_tiles, key_tiles, value_tiles, tile_lists, tile_counts):
    listed = tile_lists[tile_index]
    live_slots = jnp.arange(KMAX, dtype=jnp.int32) < tile_counts[tile_index]
    query_block = query_tiles[tile_index].astype(jnp.float32)
    key_block = key_tiles[listed].astype(jnp.float32)
    value_block = value_tiles[listed].astype(jnp.float32)
    scores = jnp.einsum('ihd,jthd->hijt', query_block, key_block, precision=lax.Precision.HIGHEST) / math.sqrt(HD)
    kept = live_slots[None, None, :, None]
    masked = jnp.where(kept, scores, masked_floor)
    row_peak = lax.optimization_barrier(jnp.max(masked, axis=(2, 3), keepdims=True))
    weights = jnp.where(kept, jnp.exp(masked - row_peak), 0.0)
    totals = lax.optimization_barrier(jnp.sum(weights, axis=(2, 3)))
    weight_rounded = lax.optimization_barrier(weights.astype(jnp.bfloat16))
    weight_wide = weight_rounded.astype(jnp.float32)
    summed = jnp.einsum('hijt,jthd->ihd', weight_wide, value_block, precision=lax.Precision.HIGHEST)
    return (summed / jnp.transpose(totals)[:, :, None]).astype(jnp.bfloat16)

def reference(queries, keys, values, out_weight, tile_lists, tile_counts):
    query_tiles = queries.reshape(NT, TILE, HEADS, HD)
    key_tiles = keys.reshape(NT, TILE, HEADS, HD)
    value_tiles = values.reshape(NT, TILE, HEADS, HD)

    def one_tile(tile_index):
        return tile_attention(tile_index, query_tiles, key_tiles, value_tiles, tile_lists, tile_counts)
    attended = lax.map(one_tile, jnp.arange(NT, dtype=jnp.int32)).reshape(TOKENS, HEADS * HD)
    group_width = HEADS * HD // GROUPS
    by_group = jnp.transpose(attended.reshape(TOKENS, GROUPS, group_width), (1, 0, 2))
    weight_groups = out_weight.reshape(GROUPS, group_width, D)

    def add_group(running, operands):
        group_term = jnp.dot(operands[0], operands[1], preferred_element_type=jnp.float32).astype(jnp.bfloat16)
        group_term = lax.optimization_barrier(group_term)
        return (running + group_term.astype(jnp.float32), None)
    running, _ = lax.scan(add_group, jnp.zeros((TOKENS, D), jnp.float32), (by_group, weight_groups))
    return running.astype(jnp.bfloat16)
```

```python
import math

import jax
import jax.numpy as jnp
from jax import lax
from jax.sharding import Mesh
from jax.sharding import PartitionSpec as P

HD = 128
TILE = 128
REACH = 5

SEQ = ("chip", "core")

masked_floor = -1e30


def shifted(x, axis, by):
    peers = lax.axis_size(axis)
    pairs = [(i, i + by) for i in range(peers) if 0 <= i + by < peers]
    return lax.ppermute(x, axis, pairs)


def swapped(x, axis):
    return lax.ppermute(x, axis, [(0, 1), (1, 0)])


def fifth_neighbour(x, chips):
    peers = chips * 2
    pairs = []
    for s in range(peers):
        t = s + REACH if s % 2 == 1 else s - REACH
        if 0 <= t < peers:
            pairs.append((s, t))
    return lax.ppermute(x, SEQ, pairs)


def local(queries, keys, values, out_weight, tile_lists, tile_counts):
    tok_rows, feat_width = queries.shape
    tiles_here = tok_rows // TILE
    heads_here = feat_width // HD
    chips = lax.axis_size("chip")
    core = lax.axis_index("core")
    device_index = lax.axis_index("chip") * 2 + core
    query_heads = queries.reshape(tok_rows, heads_here, HD)
    stacked = jnp.stack([keys, values])
    own_lists = lax.dynamic_slice_in_dim(tile_lists, device_index * tiles_here, tiles_here, 0)
    own_counts = lax.dynamic_slice_in_dim(tile_counts, device_index * tiles_here, tiles_here, 0)
    live_slots = jnp.arange(own_lists.shape[1], dtype=jnp.int32)[None, :] < own_counts[:, None]

    def tile_need(offset):
        key_tiles = (device_index + offset) * tiles_here + jnp.arange(tiles_here, dtype=jnp.int32)
        matches = (own_lists[:, :, None] == key_tiles[None, None, :]) & live_slots[:, :, None]
        return jnp.any(matches, axis=1)

    def attend(softmax_state, kv_block, token_mask):
        row_peak, totals, summed = softmax_state
        key_heads = kv_block[0].reshape(tok_rows, heads_here, HD)
        value_heads = kv_block[1].reshape(tok_rows, heads_here, HD)
        scores = jnp.einsum(
            "qhd,khd->hqk", query_heads, key_heads, preferred_element_type=jnp.float32
        ) / math.sqrt(HD)
        kept = token_mask[None]
        masked = jnp.where(kept, scores, masked_floor)
        new_peak = jnp.maximum(row_peak, jnp.max(masked, axis=2))
        carried = jnp.exp(row_peak - new_peak)
        weights = jnp.where(kept, jnp.exp(masked - new_peak[:, :, None]), 0.0)
        totals = carried * totals + jnp.sum(weights, axis=2)
        weight_rounded = weights.astype(jnp.bfloat16)
        summed = carried[:, :, None] * summed + jnp.einsum(
            "hqk,khd->hqd", weight_rounded, value_heads, preferred_element_type=jnp.float32
        )
        return (new_peak, totals, summed)

    kv_blocks = []
    sibling = swapped(stacked, "core")
    kv_blocks.append((1 - 2 * core, sibling))
    kv_blocks.append((-REACH + 2 * REACH * core, fifth_neighbour(stacked, chips)))
    fetched = []
    for chip_step in (1, 2):
        for sign in (1, -1):
            block = shifted(stacked, "chip", sign * chip_step)
            fetched.append((-sign * 2 * chip_step, block))
            kv_blocks.append((-sign * 2 * chip_step, block))
    for offset, block in fetched:
        passed = swapped(block, "core")
        kv_blocks.append((offset + 1 - 2 * core, passed))

    def expand(tile_mask):
        return jnp.repeat(jnp.repeat(tile_mask, TILE, axis=0), TILE, axis=1)

    softmax_state = (
        jnp.full((heads_here, tok_rows), masked_floor, jnp.float32),
        jnp.zeros((heads_here, tok_rows), jnp.float32),
        jnp.zeros((heads_here, tok_rows, HD), jnp.float32),
    )
    softmax_state = attend(softmax_state, stacked, expand(tile_need(0)))
    for offset, kv_block in kv_blocks:
        tile_mask = tile_need(offset)
        token_mask = expand(tile_mask)

        def taken(carry, kv_block=kv_block, token_mask=token_mask):
            return attend(carry, kv_block, token_mask)

        def skipped(carry):
            return carry

        softmax_state = lax.cond(jnp.any(tile_mask), taken, skipped, softmax_state)
    row_peak, totals, summed = softmax_state
    attended = (
        jnp.transpose(summed / totals[:, :, None], (1, 0, 2))
        .reshape(tok_rows, feat_width)
        .astype(jnp.bfloat16)
    )
    weight_rows = lax.all_gather(out_weight, SEQ, axis=1, tiled=True)
    heads = lax.axis_size("head")
    if heads == 2:
        half = weight_rows.shape[1] // 2
        me = lax.axis_index("head")
        mine = lax.dynamic_slice_in_dim(weight_rows, me * half, half, 1)
        theirs = lax.dynamic_slice_in_dim(weight_rows, (1 - me) * half, half, 1)
        sent = jnp.dot(attended, theirs, preferred_element_type=jnp.float32).astype(jnp.bfloat16)
        got = swapped(sent, "head")
        kept_part = jnp.dot(attended, mine, preferred_element_type=jnp.float32).astype(jnp.bfloat16)
        return (kept_part.astype(jnp.float32) + got.astype(jnp.float32)).astype(jnp.bfloat16)
    projected = jnp.dot(attended, weight_rows, preferred_element_type=jnp.float32)
    return lax.psum_scatter(projected.astype(jnp.bfloat16), "head", scatter_dimension=1, tiled=True)


def solution(mesh):
    heads = mesh.shape["head"]
    seq = mesh.shape["seq"]
    view = Mesh(mesh.devices.reshape(heads, seq // 2, 2), ("head", "chip", "core"))
    return jax.shard_map(
        local,
        mesh=view,
        in_specs=(P(SEQ, "head"), P(SEQ, "head"), P(SEQ, "head"), P("head", SEQ), P(), P()),
        out_specs=P(SEQ, "head"),
        check_vma=False,
    )
```

```python
import functools
import math

import jax
import jax.numpy as jnp
from jax import lax
from jax.experimental import pallas as pl
from jax.experimental.pallas import tpu as pltpu
from jax.sharding import Mesh
from jax.sharding import PartitionSpec as P

HD = 128
TILE = 128
REACH = 5

SEQ = ("chip", "core")

masked_floor = -1e30


def shifted(x, axis, by):
    peers = lax.axis_size(axis)
    pairs = [(i, i + by) for i in range(peers) if 0 <= i + by < peers]
    return lax.ppermute(x, axis, pairs)


def swapped(x, axis):
    return lax.ppermute(x, axis, [(0, 1), (1, 0)])


def fifth_neighbour(x, chips):
    peers = chips * 2
    pairs = []
    for s in range(peers):
        t = s + REACH if s % 2 == 1 else s - REACH
        if 0 <= t < peers:
            pairs.append((s, t))
    return lax.ppermute(x, SEQ, pairs)


def attention_kernel(n_blocks, tiles, mask_ref, q_ref, *refs):
    kv_refs = refs[:n_blocks]
    out_ref = refs[n_blocks]
    score_ref = refs[n_blocks + 1]
    rows = q_ref.shape[0]
    query = q_ref[...]
    for b in range(n_blocks):
        keys = kv_refs[b][0]
        scores = lax.dot_general(
            query, keys, (((1,), (1,)), ((), ())), preferred_element_type=jnp.float32
        ) / math.sqrt(HD)
        score_ref[:, b * rows:(b + 1) * rows] = scores
        for qi in range(tiles):
            for kt in range(tiles):
                flag = mask_ref[(b * tiles + qi) * tiles + kt]

                @pl.when(flag == 0)
                def _(b=b, qi=qi, kt=kt):
                    score_ref[qi * TILE:(qi + 1) * TILE, b * rows + kt * TILE:b * rows + (kt + 1) * TILE] = (
                        jnp.full((TILE, TILE), masked_floor, jnp.float32)
                    )

    scores = score_ref[...]
    peak = jnp.max(scores, axis=1, keepdims=True)
    weights = jnp.exp(scores - peak)
    totals = jnp.sum(weights, axis=1, keepdims=True)
    rounded = weights.astype(jnp.bfloat16)
    summed = jnp.zeros((rows, HD), jnp.float32)
    for b in range(n_blocks):
        summed = summed + jnp.dot(
            rounded[:, b * rows:(b + 1) * rows], kv_refs[b][1], preferred_element_type=jnp.float32
        )
    out_ref[...] = (summed / totals).astype(out_ref.dtype)


def block_attention(queries, kv_list, flat_masks):
    rows, width = queries.shape
    heads = width // HD
    n_blocks = len(kv_list)
    tiles = rows // TILE
    kv_spec = pl.BlockSpec((2, rows, HD), lambda h, m: (0, 0, h))
    grid_spec = pltpu.PrefetchScalarGridSpec(
        num_scalar_prefetch=1,
        grid=(heads,),
        in_specs=[pl.BlockSpec((rows, HD), lambda h, m: (0, h))] + [kv_spec] * n_blocks,
        out_specs=pl.BlockSpec((rows, HD), lambda h, m: (0, h)),
        scratch_shapes=[pltpu.VMEM((rows, n_blocks * rows), jnp.float32)],
    )
    flops = 4 * rows * n_blocks * rows * HD * heads
    bytes_moved = 2 * (rows * width * 2 + n_blocks * 2 * rows * width)
    return pl.pallas_call(
        functools.partial(attention_kernel, n_blocks, tiles),
        grid_spec=grid_spec,
        out_shape=jax.ShapeDtypeStruct((rows, width), jnp.bfloat16),
        cost_estimate=pl.CostEstimate(
            flops=flops, transcendentals=rows * n_blocks * rows * heads, bytes_accessed=bytes_moved
        ),
    )(flat_masks, queries, *kv_list)


def local(queries, keys, values, out_weight, tile_lists, tile_counts):
    tok_rows, feat_width = queries.shape
    tiles_here = tok_rows // TILE
    heads_here = feat_width // HD
    chips = lax.axis_size("chip")
    core = lax.axis_index("core")
    device_index = lax.axis_index("chip") * 2 + core
    query_heads = queries.reshape(tok_rows, heads_here, HD)
    stacked = jnp.stack([keys, values])
    own_lists = lax.dynamic_slice_in_dim(tile_lists, device_index * tiles_here, tiles_here, 0)
    own_counts = lax.dynamic_slice_in_dim(tile_counts, device_index * tiles_here, tiles_here, 0)
    live_slots = jnp.arange(own_lists.shape[1], dtype=jnp.int32)[None, :] < own_counts[:, None]

    def tile_need(offset):
        key_tiles = (device_index + offset) * tiles_here + jnp.arange(tiles_here, dtype=jnp.int32)
        matches = (own_lists[:, :, None] == key_tiles[None, None, :]) & live_slots[:, :, None]
        return jnp.any(matches, axis=1)

    kv_blocks = [(0, stacked)]
    sibling = swapped(stacked, "core")
    kv_blocks.append((1 - 2 * core, sibling))
    kv_blocks.append((-REACH + 2 * REACH * core, fifth_neighbour(stacked, chips)))
    fetched = []
    for chip_step in (1, 2):
        for sign in (1, -1):
            block = shifted(stacked, "chip", sign * chip_step)
            fetched.append((-sign * 2 * chip_step, block))
            kv_blocks.append((-sign * 2 * chip_step, block))
    for offset, block in fetched:
        passed = swapped(block, "core")
        kv_blocks.append((offset + 1 - 2 * core, passed))

    tile_masks = jnp.stack([tile_need(offset) for offset, _ in kv_blocks]).astype(jnp.int32)
    attended = block_attention(queries, [b for _, b in kv_blocks], tile_masks.reshape(-1))
    weight_rows = lax.all_gather(out_weight, SEQ, axis=1, tiled=True)
    heads = lax.axis_size("head")
    if heads == 2:
        half = weight_rows.shape[1] // 2
        me = lax.axis_index("head")
        mine = lax.dynamic_slice_in_dim(weight_rows, me * half, half, 1)
        theirs = lax.dynamic_slice_in_dim(weight_rows, (1 - me) * half, half, 1)
        sent = jnp.dot(attended, theirs, preferred_element_type=jnp.float32).astype(jnp.bfloat16)
        got = swapped(sent, "head")
        kept_part = jnp.dot(attended, mine, preferred_element_type=jnp.float32).astype(jnp.bfloat16)
        kept_part = lax.optimization_barrier(kept_part)
        return (kept_part.astype(jnp.float32) + got.astype(jnp.float32)).astype(jnp.bfloat16)
    projected = jnp.dot(attended, weight_rows, preferred_element_type=jnp.float32)
    return lax.psum_scatter(projected.astype(jnp.bfloat16), "head", scatter_dimension=1, tiled=True)


def solution(mesh):
    heads = mesh.shape["head"]
    seq = mesh.shape["seq"]
    view = Mesh(mesh.devices.reshape(heads, seq // 2, 2), ("head", "chip", "core"))
    return jax.shard_map(
        local,
        mesh=view,
        in_specs=(P(SEQ, "head"), P(SEQ, "head"), P(SEQ, "head"), P("head", SEQ), P(), P()),
        out_specs=P(SEQ, "head"),
        check_vma=False,
    )
```

```python
import functools
import math

import jax
import jax.numpy as jnp
from jax import lax
from jax.experimental import pallas as pl
from jax.experimental.pallas import tpu as pltpu
from jax.sharding import Mesh
from jax.sharding import PartitionSpec as P

HD = 128
TILE = 128
REACH = 5

SEQ = ("chip", "core")

masked_floor = -1e30


def shifted(x, axis, by):
    peers = lax.axis_size(axis)
    pairs = [(i, i + by) for i in range(peers) if 0 <= i + by < peers]
    return lax.ppermute(x, axis, pairs)


def swapped(x, axis):
    return lax.ppermute(x, axis, [(0, 1), (1, 0)])


def fifth_neighbour(x, chips):
    peers = chips * 2
    pairs = []
    for s in range(peers):
        t = s + REACH if s % 2 == 1 else s - REACH
        if 0 <= t < peers:
            pairs.append((s, t))
    return lax.ppermute(x, SEQ, pairs)


def attention_kernel(n_blocks, tiles, group, mask_ref, q_ref, *refs):
    kv_refs = refs[:n_blocks]
    out_ref = refs[n_blocks]
    score_ref = refs[n_blocks + 1]
    rows = q_ref.shape[0]
    for g in range(group):
        cols = slice(g * HD, (g + 1) * HD)
        query = q_ref[:, cols]
        for b in range(n_blocks):
            keys = kv_refs[b][0, :, cols]
            scores = lax.dot_general(
                query, keys, (((1,), (1,)), ((), ())), preferred_element_type=jnp.float32
            ) / math.sqrt(HD)
            score_ref[:, b * rows:(b + 1) * rows] = scores
            for qi in range(tiles):
                for kt in range(tiles):
                    flag = mask_ref[(b * tiles + qi) * tiles + kt]

                    @pl.when(flag == 0)
                    def _(b=b, qi=qi, kt=kt):
                        score_ref[qi * TILE:(qi + 1) * TILE, b * rows + kt * TILE:b * rows + (kt + 1) * TILE] = (
                            jnp.full((TILE, TILE), masked_floor, jnp.float32)
                        )

        scores = score_ref[...]
        peak = jnp.max(scores, axis=1, keepdims=True)
        weights = jnp.exp(scores - peak)
        totals = jnp.sum(weights, axis=1, keepdims=True)
        rounded = weights.astype(jnp.bfloat16)
        summed = jnp.zeros((rows, HD), jnp.float32)
        for b in range(n_blocks):
            summed = summed + jnp.dot(
                rounded[:, b * rows:(b + 1) * rows], kv_refs[b][1, :, cols], preferred_element_type=jnp.float32
            )
        out_ref[:, cols] = (summed / totals).astype(out_ref.dtype)


def block_attention(queries, kv_list, flat_masks):
    rows, width = queries.shape
    heads = width // HD
    group = 5 if heads % 5 == 0 else 1
    n_blocks = len(kv_list)
    tiles = rows // TILE
    span = group * HD
    kv_spec = pl.BlockSpec((2, rows, span), lambda h, m: (0, 0, h))
    grid_spec = pltpu.PrefetchScalarGridSpec(
        num_scalar_prefetch=1,
        grid=(heads // group,),
        in_specs=[pl.BlockSpec((rows, span), lambda h, m: (0, h))] + [kv_spec] * n_blocks,
        out_specs=pl.BlockSpec((rows, span), lambda h, m: (0, h)),
        scratch_shapes=[pltpu.VMEM((rows, n_blocks * rows), jnp.float32)],
    )
    flops = 4 * rows * n_blocks * rows * HD * heads
    bytes_moved = 2 * (rows * width * 2 + n_blocks * 2 * rows * width)
    return pl.pallas_call(
        functools.partial(attention_kernel, n_blocks, tiles, group),
        grid_spec=grid_spec,
        out_shape=jax.ShapeDtypeStruct((rows, width), jnp.bfloat16),
        cost_estimate=pl.CostEstimate(
            flops=flops, transcendentals=rows * n_blocks * rows * heads, bytes_accessed=bytes_moved
        ),
    )(flat_masks, queries, *kv_list)


def local(queries, keys, values, out_weight, tile_lists, tile_counts):
    tok_rows, feat_width = queries.shape
    tiles_here = tok_rows // TILE
    heads_here = feat_width // HD
    chips = lax.axis_size("chip")
    core = lax.axis_index("core")
    device_index = lax.axis_index("chip") * 2 + core
    query_heads = queries.reshape(tok_rows, heads_here, HD)
    stacked = jnp.stack([keys, values])
    own_lists = lax.dynamic_slice_in_dim(tile_lists, device_index * tiles_here, tiles_here, 0)
    own_counts = lax.dynamic_slice_in_dim(tile_counts, device_index * tiles_here, tiles_here, 0)
    live_slots = jnp.arange(own_lists.shape[1], dtype=jnp.int32)[None, :] < own_counts[:, None]

    def tile_need(offset):
        key_tiles = (device_index + offset) * tiles_here + jnp.arange(tiles_here, dtype=jnp.int32)
        matches = (own_lists[:, :, None] == key_tiles[None, None, :]) & live_slots[:, :, None]
        return jnp.any(matches, axis=1)

    kv_blocks = [(0, stacked)]
    sibling = swapped(stacked, "core")
    kv_blocks.append((1 - 2 * core, sibling))
    kv_blocks.append((-REACH + 2 * REACH * core, fifth_neighbour(stacked, chips)))
    fetched = []
    for chip_step in (1, 2):
        for sign in (1, -1):
            block = shifted(stacked, "chip", sign * chip_step)
            fetched.append((-sign * 2 * chip_step, block))
            kv_blocks.append((-sign * 2 * chip_step, block))
    for offset, block in fetched:
        passed = swapped(block, "core")
        kv_blocks.append((offset + 1 - 2 * core, passed))

    tile_masks = jnp.stack([tile_need(offset) for offset, _ in kv_blocks]).astype(jnp.int32)
    attended = block_attention(queries, [b for _, b in kv_blocks], tile_masks.reshape(-1))
    weight_rows = lax.all_gather(out_weight, SEQ, axis=1, tiled=True)
    heads = lax.axis_size("head")
    if heads == 2:
        half = weight_rows.shape[1] // 2
        me = lax.axis_index("head")
        mine = lax.dynamic_slice_in_dim(weight_rows, me * half, half, 1)
        theirs = lax.dynamic_slice_in_dim(weight_rows, (1 - me) * half, half, 1)
        sent = jnp.dot(attended, theirs, preferred_element_type=jnp.float32).astype(jnp.bfloat16)
        got = swapped(sent, "head")
        kept_part = jnp.dot(attended, mine, preferred_element_type=jnp.float32).astype(jnp.bfloat16)
        kept_part = lax.optimization_barrier(kept_part)
        return (kept_part.astype(jnp.float32) + got.astype(jnp.float32)).astype(jnp.bfloat16)
    projected = jnp.dot(attended, weight_rows, preferred_element_type=jnp.float32)
    return lax.psum_scatter(projected.astype(jnp.bfloat16), "head", scatter_dimension=1, tiled=True)


def solution(mesh):
    heads = mesh.shape["head"]
    seq = mesh.shape["seq"]
    view = Mesh(mesh.devices.reshape(heads, seq // 2, 2), ("head", "chip", "core"))
    return jax.shard_map(
        local,
        mesh=view,
        in_specs=(P(SEQ, "head"), P(SEQ, "head"), P(SEQ, "head"), P("head", SEQ), P(), P()),
        out_specs=P(SEQ, "head"),
        check_vma=False,
    )
```

```python
import functools
import math

import jax
import jax.numpy as jnp
from jax import lax
from jax.experimental import pallas as pl
from jax.experimental.pallas import tpu as pltpu
from jax.sharding import Mesh
from jax.sharding import PartitionSpec as P

HD = 128
TILE = 128
REACH = 5

SEQ = ("chip", "core")

masked_floor = -1e30


def shifted(x, axis, by):
    peers = lax.axis_size(axis)
    pairs = [(i, i + by) for i in range(peers) if 0 <= i + by < peers]
    return lax.ppermute(x, axis, pairs)


def swapped(x, axis):
    return lax.ppermute(x, axis, [(0, 1), (1, 0)])


def fifth_neighbour(x, chips):
    peers = chips * 2
    pairs = []
    for s in range(peers):
        t = s + REACH if s % 2 == 1 else s - REACH
        if 0 <= t < peers:
            pairs.append((s, t))
    return lax.ppermute(x, SEQ, pairs)


def attention_kernel(n_blocks, tiles, group, mask_ref, q_ref, *refs):
    kv_refs = refs[:n_blocks]
    out_ref = refs[n_blocks]
    score_ref, peak_ref, total_ref, acc_ref = refs[n_blocks + 1:]
    rows = q_ref.shape[0]
    listed = [
        (b, qi, kt)
        for b in range(n_blocks)
        for qi in range(tiles)
        for kt in range(tiles)
    ]

    def one_head(g, carry):
        cols = pl.ds(pl.multiple_of(g * HD, HD), HD)
        peak_ref[...] = jnp.full(peak_ref.shape, masked_floor, jnp.float32)
        total_ref[...] = jnp.zeros(total_ref.shape, jnp.float32)
        acc_ref[...] = jnp.zeros(acc_ref.shape, jnp.float32)
        for b, qi, kt in listed:
            flag = mask_ref[(b * tiles + qi) * tiles + kt]

            @pl.when(flag != 0)
            def _(b=b, qi=qi, kt=kt):
                q_rows = slice(qi * TILE, (qi + 1) * TILE)
                query = q_ref[q_rows, cols]
                keys = kv_refs[b][0, kt * TILE:(kt + 1) * TILE, cols]
                scores = lax.dot_general(
                    query, keys, (((1,), (1,)), ((), ())), preferred_element_type=jnp.float32
                ) / math.sqrt(HD)
                score_ref[q_rows, (b * tiles + kt) * TILE:(b * tiles + kt + 1) * TILE] = scores
                peak_ref[q_rows, :] = jnp.maximum(peak_ref[q_rows, :], jnp.max(scores, axis=1, keepdims=True))

        for b, qi, kt in listed:
            flag = mask_ref[(b * tiles + qi) * tiles + kt]

            @pl.when(flag != 0)
            def _(b=b, qi=qi, kt=kt):
                q_rows = slice(qi * TILE, (qi + 1) * TILE)
                scores = score_ref[q_rows, (b * tiles + kt) * TILE:(b * tiles + kt + 1) * TILE]
                weights = jnp.exp(scores - peak_ref[q_rows, :])
                total_ref[q_rows, :] += jnp.sum(weights, axis=1, keepdims=True)
                acc_ref[q_rows, :] += jnp.dot(
                    weights.astype(jnp.bfloat16),
                    kv_refs[b][1, kt * TILE:(kt + 1) * TILE, cols],
                    preferred_element_type=jnp.float32,
                )

        out_ref[:, cols] = (acc_ref[...] / total_ref[...]).astype(out_ref.dtype)
        return carry

    lax.fori_loop(0, group, one_head, 0)


def block_attention(queries, kv_list, flat_masks):
    rows, width = queries.shape
    heads = width // HD
    group = 5 if heads % 5 == 0 else 1
    n_blocks = len(kv_list)
    tiles = rows // TILE
    span = group * HD
    kv_spec = pl.BlockSpec((2, rows, span), lambda h, m: (0, 0, h))
    grid_spec = pltpu.PrefetchScalarGridSpec(
        num_scalar_prefetch=1,
        grid=(heads // group,),
        in_specs=[pl.BlockSpec((rows, span), lambda h, m: (0, h))] + [kv_spec] * n_blocks,
        out_specs=pl.BlockSpec((rows, span), lambda h, m: (0, h)),
        scratch_shapes=[
            pltpu.VMEM((rows, n_blocks * rows), jnp.float32),
            pltpu.VMEM((rows, 1), jnp.float32),
            pltpu.VMEM((rows, 1), jnp.float32),
            pltpu.VMEM((rows, HD), jnp.float32),
        ],
    )
    flops = 4 * rows * n_blocks * rows * HD * heads
    bytes_moved = 2 * (rows * width * 2 + n_blocks * 2 * rows * width)
    return pl.pallas_call(
        functools.partial(attention_kernel, n_blocks, tiles, group),
        grid_spec=grid_spec,
        out_shape=jax.ShapeDtypeStruct((rows, width), jnp.bfloat16),
        cost_estimate=pl.CostEstimate(
            flops=flops, transcendentals=rows * n_blocks * rows * heads, bytes_accessed=bytes_moved
        ),
    )(flat_masks, queries, *kv_list)


def local(queries, keys, values, out_weight, tile_lists, tile_counts):
    tok_rows, feat_width = queries.shape
    tiles_here = tok_rows // TILE
    heads_here = feat_width // HD
    chips = lax.axis_size("chip")
    core = lax.axis_index("core")
    device_index = lax.axis_index("chip") * 2 + core
    query_heads = queries.reshape(tok_rows, heads_here, HD)
    stacked = jnp.stack([keys, values])
    own_lists = lax.dynamic_slice_in_dim(tile_lists, device_index * tiles_here, tiles_here, 0)
    own_counts = lax.dynamic_slice_in_dim(tile_counts, device_index * tiles_here, tiles_here, 0)
    live_slots = jnp.arange(own_lists.shape[1], dtype=jnp.int32)[None, :] < own_counts[:, None]

    def tile_need(offset):
        key_tiles = (device_index + offset) * tiles_here + jnp.arange(tiles_here, dtype=jnp.int32)
        matches = (own_lists[:, :, None] == key_tiles[None, None, :]) & live_slots[:, :, None]
        return jnp.any(matches, axis=1)

    kv_blocks = [(0, stacked)]
    sibling = swapped(stacked, "core")
    kv_blocks.append((1 - 2 * core, sibling))
    kv_blocks.append((-REACH + 2 * REACH * core, fifth_neighbour(stacked, chips)))
    fetched = []
    for chip_step in (1, 2):
        for sign in (1, -1):
            block = shifted(stacked, "chip", sign * chip_step)
            fetched.append((-sign * 2 * chip_step, block))
            kv_blocks.append((-sign * 2 * chip_step, block))
    for offset, block in fetched:
        passed = swapped(block, "core")
        kv_blocks.append((offset + 1 - 2 * core, passed))

    tile_masks = jnp.stack([tile_need(offset) for offset, _ in kv_blocks]).astype(jnp.int32)
    attended = block_attention(queries, [b for _, b in kv_blocks], tile_masks.reshape(-1))
    weight_rows = lax.all_gather(out_weight, SEQ, axis=1, tiled=True)
    heads = lax.axis_size("head")
    if heads == 2:
        half = weight_rows.shape[1] // 2
        me = lax.axis_index("head")
        mine = lax.dynamic_slice_in_dim(weight_rows, me * half, half, 1)
        theirs = lax.dynamic_slice_in_dim(weight_rows, (1 - me) * half, half, 1)
        sent = jnp.dot(attended, theirs, preferred_element_type=jnp.float32).astype(jnp.bfloat16)
        got = swapped(sent, "head")
        kept_part = jnp.dot(attended, mine, preferred_element_type=jnp.float32).astype(jnp.bfloat16)
        kept_part = lax.optimization_barrier(kept_part)
        return (kept_part.astype(jnp.float32) + got.astype(jnp.float32)).astype(jnp.bfloat16)
    projected = jnp.dot(attended, weight_rows, preferred_element_type=jnp.float32)
    return lax.psum_scatter(projected.astype(jnp.bfloat16), "head", scatter_dimension=1, tiled=True)


def solution(mesh):
    heads = mesh.shape["head"]
    seq = mesh.shape["seq"]
    view = Mesh(mesh.devices.reshape(heads, seq // 2, 2), ("head", "chip", "core"))
    return jax.shard_map(
        local,
        mesh=view,
        in_specs=(P(SEQ, "head"), P(SEQ, "head"), P(SEQ, "head"), P("head", SEQ), P(), P()),
        out_specs=P(SEQ, "head"),
        check_vma=False,
    )
```

```python
import functools
import math

import jax
import jax.numpy as jnp
from jax import lax
from jax.experimental import pallas as pl
from jax.experimental.pallas import tpu as pltpu
from jax.sharding import Mesh
from jax.sharding import PartitionSpec as P

HD = 128
TILE = 128
REACH = 5

SEQ = ("chip", "core")

masked_floor = -1e30


def shifted(x, axis, by):
    peers = lax.axis_size(axis)
    pairs = [(i, i + by) for i in range(peers) if 0 <= i + by < peers]
    return lax.ppermute(x, axis, pairs)


def swapped(x, axis):
    return lax.ppermute(x, axis, [(0, 1), (1, 0)])


def fifth_neighbour(x, chips):
    peers = chips * 2
    pairs = []
    for s in range(peers):
        t = s + REACH if s % 2 == 1 else s - REACH
        if 0 <= t < peers:
            pairs.append((s, t))
    return lax.ppermute(x, SEQ, pairs)


def attention_kernel(n_blocks, tiles, group, mask_ref, q_ref, *refs):
    kv_refs = refs[:n_blocks]
    out_ref = refs[n_blocks]
    score_ref = refs[n_blocks + 1]
    rows = q_ref.shape[0]
    for g in range(group):
        cols = slice(g * HD, (g + 1) * HD)
        query = q_ref[:, cols]
        for b in range(n_blocks):
            keys = kv_refs[b][0, :, cols]
            scores = lax.dot_general(
                query, keys, (((1,), (1,)), ((), ())), preferred_element_type=jnp.float32
            ) * (1.0 / math.sqrt(HD))
            for qi in range(tiles):
                for kt in range(tiles):
                    flag = mask_ref[(b * tiles + qi) * tiles + kt]
                    tile = scores[qi * TILE:(qi + 1) * TILE, kt * TILE:(kt + 1) * TILE]
                    score_ref[qi * TILE:(qi + 1) * TILE, b * rows + kt * TILE:b * rows + (kt + 1) * TILE] = (
                        jnp.where(flag != 0, tile, masked_floor)
                    )

        scores = score_ref[...]
        peak = jnp.max(scores, axis=1, keepdims=True)
        weights = jnp.exp(scores - peak)
        totals = jnp.sum(weights, axis=1, keepdims=True)
        rounded = weights.astype(jnp.bfloat16)
        summed = jnp.zeros((rows, HD), jnp.float32)
        for b in range(n_blocks):
            summed = summed + jnp.dot(
                rounded[:, b * rows:(b + 1) * rows], kv_refs[b][1, :, cols], preferred_element_type=jnp.float32
            )
        out_ref[:, cols] = (summed / totals).astype(out_ref.dtype)


def block_attention(queries, kv_list, flat_masks):
    rows, width = queries.shape
    heads = width // HD
    group = 5 if heads % 5 == 0 else 1
    n_blocks = len(kv_list)
    tiles = rows // TILE
    span = group * HD
    kv_spec = pl.BlockSpec((2, rows, span), lambda h, m: (0, 0, h))
    grid_spec = pltpu.PrefetchScalarGridSpec(
        num_scalar_prefetch=1,
        grid=(heads // group,),
        in_specs=[pl.BlockSpec((rows, span), lambda h, m: (0, h))] + [kv_spec] * n_blocks,
        out_specs=pl.BlockSpec((rows, span), lambda h, m: (0, h)),
        scratch_shapes=[pltpu.VMEM((rows, n_blocks * rows), jnp.float32)],
    )
    flops = 4 * rows * n_blocks * rows * HD * heads
    bytes_moved = 2 * (rows * width * 2 + n_blocks * 2 * rows * width)
    return pl.pallas_call(
        functools.partial(attention_kernel, n_blocks, tiles, group),
        grid_spec=grid_spec,
        out_shape=jax.ShapeDtypeStruct((rows, width), jnp.bfloat16),
        cost_estimate=pl.CostEstimate(
            flops=flops, transcendentals=rows * n_blocks * rows * heads, bytes_accessed=bytes_moved
        ),
    )(flat_masks, queries, *kv_list)


def local(queries, keys, values, out_weight, tile_lists, tile_counts):
    tok_rows, feat_width = queries.shape
    tiles_here = tok_rows // TILE
    heads_here = feat_width // HD
    chips = lax.axis_size("chip")
    core = lax.axis_index("core")
    device_index = lax.axis_index("chip") * 2 + core
    query_heads = queries.reshape(tok_rows, heads_here, HD)
    stacked = jnp.stack([keys, values])
    own_lists = lax.dynamic_slice_in_dim(tile_lists, device_index * tiles_here, tiles_here, 0)
    own_counts = lax.dynamic_slice_in_dim(tile_counts, device_index * tiles_here, tiles_here, 0)
    live_slots = jnp.arange(own_lists.shape[1], dtype=jnp.int32)[None, :] < own_counts[:, None]

    def tile_need(offset):
        key_tiles = (device_index + offset) * tiles_here + jnp.arange(tiles_here, dtype=jnp.int32)
        matches = (own_lists[:, :, None] == key_tiles[None, None, :]) & live_slots[:, :, None]
        return jnp.any(matches, axis=1)

    kv_blocks = [(0, stacked)]
    sibling = swapped(stacked, "core")
    kv_blocks.append((1 - 2 * core, sibling))
    kv_blocks.append((-REACH + 2 * REACH * core, fifth_neighbour(stacked, chips)))
    fetched = []
    for chip_step in (1, 2):
        for sign in (1, -1):
            block = shifted(stacked, "chip", sign * chip_step)
            fetched.append((-sign * 2 * chip_step, block))
            kv_blocks.append((-sign * 2 * chip_step, block))
    for offset, block in fetched:
        passed = swapped(block, "core")
        kv_blocks.append((offset + 1 - 2 * core, passed))

    tile_masks = jnp.stack([tile_need(offset) for offset, _ in kv_blocks]).astype(jnp.int32)
    attended = block_attention(queries, [b for _, b in kv_blocks], tile_masks.reshape(-1))
    weight_rows = lax.all_gather(out_weight, SEQ, axis=1, tiled=True)
    heads = lax.axis_size("head")
    if heads == 2:
        half = weight_rows.shape[1] // 2
        me = lax.axis_index("head")
        mine = lax.dynamic_slice_in_dim(weight_rows, me * half, half, 1)
        theirs = lax.dynamic_slice_in_dim(weight_rows, (1 - me) * half, half, 1)
        sent = jnp.dot(attended, theirs, preferred_element_type=jnp.float32).astype(jnp.bfloat16)
        got = swapped(sent, "head")
        kept_part = jnp.dot(attended, mine, preferred_element_type=jnp.float32).astype(jnp.bfloat16)
        kept_part = lax.optimization_barrier(kept_part)
        return (kept_part.astype(jnp.float32) + got.astype(jnp.float32)).astype(jnp.bfloat16)
    projected = jnp.dot(attended, weight_rows, preferred_element_type=jnp.float32)
    return lax.psum_scatter(projected.astype(jnp.bfloat16), "head", scatter_dimension=1, tiled=True)


def solution(mesh):
    heads = mesh.shape["head"]
    seq = mesh.shape["seq"]
    view = Mesh(mesh.devices.reshape(heads, seq // 2, 2), ("head", "chip", "core"))
    return jax.shard_map(
        local,
        mesh=view,
        in_specs=(P(SEQ, "head"), P(SEQ, "head"), P(SEQ, "head"), P("head", SEQ), P(), P()),
        out_specs=P(SEQ, "head"),
        check_vma=False,
    )
```

```python
import functools
import math

import jax
import jax.numpy as jnp
from jax import lax
from jax.experimental import pallas as pl
from jax.experimental.pallas import tpu as pltpu
from jax.sharding import Mesh
from jax.sharding import PartitionSpec as P

HD = 128
TILE = 128
REACH = 5

SEQ = ("chip", "core")

masked_floor = -1e30


def shifted(x, axis, by):
    peers = lax.axis_size(axis)
    pairs = [(i, i + by) for i in range(peers) if 0 <= i + by < peers]
    return lax.ppermute(x, axis, pairs)


def swapped(x, axis):
    return lax.ppermute(x, axis, [(0, 1), (1, 0)])


def fifth_neighbour(x, chips):
    peers = chips * 2
    pairs = []
    for s in range(peers):
        t = s + REACH if s % 2 == 1 else s - REACH
        if 0 <= t < peers:
            pairs.append((s, t))
    return lax.ppermute(x, SEQ, pairs)


def attention_kernel(n_blocks, tiles, group, mask_ref, q_ref, *refs):
    kv_refs = refs[:n_blocks]
    out_ref = refs[n_blocks]
    score_ref = refs[n_blocks + 1]
    rows = q_ref.shape[0]
    for g in range(group):
        cols = slice(g * HD, (g + 1) * HD)
        query = q_ref[:, cols]
        for b in range(n_blocks):
            keys = kv_refs[b][0, :, cols]
            scores = lax.dot_general(
                query, keys, (((1,), (1,)), ((), ())), preferred_element_type=jnp.float32
            ) * (1.0 / math.sqrt(HD))
            for qi in range(tiles):
                for kt in range(tiles):
                    flag = mask_ref[(b * tiles + qi) * tiles + kt]
                    tile = scores[qi * TILE:(qi + 1) * TILE, kt * TILE:(kt + 1) * TILE]
                    score_ref[qi * TILE:(qi + 1) * TILE, b * rows + kt * TILE:b * rows + (kt + 1) * TILE] = (
                        jnp.where(flag != 0, tile, masked_floor)
                    )

        scores = score_ref[...]
        peak = jnp.max(scores, axis=1, keepdims=True)
        weights = jnp.exp(scores - peak)
        totals = jnp.sum(weights, axis=1, keepdims=True)
        rounded = weights.astype(jnp.bfloat16)
        summed = jnp.zeros((rows, HD), jnp.float32)
        for b in range(n_blocks):
            summed = summed + jnp.dot(
                rounded[:, b * rows:(b + 1) * rows], kv_refs[b][1, :, cols], preferred_element_type=jnp.float32
            )
        out_ref[:, cols] = (summed / totals).astype(out_ref.dtype)


def block_attention(queries, kv_list, flat_masks):
    rows, width = queries.shape
    heads = width // HD
    group = 5 if heads % 5 == 0 else 1
    n_blocks = len(kv_list)
    tiles = rows // TILE
    span = group * HD
    kv_spec = pl.BlockSpec((2, rows, span), lambda h, m: (0, 0, h))
    grid_spec = pltpu.PrefetchScalarGridSpec(
        num_scalar_prefetch=1,
        grid=(heads // group,),
        in_specs=[pl.BlockSpec((rows, span), lambda h, m: (0, h))] + [kv_spec] * n_blocks,
        out_specs=pl.BlockSpec((rows, span), lambda h, m: (0, h)),
        scratch_shapes=[pltpu.VMEM((rows, n_blocks * rows), jnp.float32)],
    )
    flops = 4 * rows * n_blocks * rows * HD * heads
    bytes_moved = 2 * (rows * width * 2 + n_blocks * 2 * rows * width)
    return pl.pallas_call(
        functools.partial(attention_kernel, n_blocks, tiles, group),
        grid_spec=grid_spec,
        out_shape=jax.ShapeDtypeStruct((rows, width), jnp.bfloat16),
        cost_estimate=pl.CostEstimate(
            flops=flops, transcendentals=rows * n_blocks * rows * heads, bytes_accessed=bytes_moved
        ),
    )(flat_masks, queries, *kv_list)


def local(queries, keys, values, out_weight, tile_lists, tile_counts):
    tok_rows, feat_width = queries.shape
    tiles_here = tok_rows // TILE
    heads_here = feat_width // HD
    chips = lax.axis_size("chip")
    core = lax.axis_index("core")
    device_index = lax.axis_index("chip") * 2 + core
    query_heads = queries.reshape(tok_rows, heads_here, HD)
    stacked = jnp.stack([keys, values])
    own_lists = lax.dynamic_slice_in_dim(tile_lists, device_index * tiles_here, tiles_here, 0)
    own_counts = lax.dynamic_slice_in_dim(tile_counts, device_index * tiles_here, tiles_here, 0)
    live_slots = jnp.arange(own_lists.shape[1], dtype=jnp.int32)[None, :] < own_counts[:, None]

    def tile_need(offset):
        key_tiles = (device_index + offset) * tiles_here + jnp.arange(tiles_here, dtype=jnp.int32)
        matches = (own_lists[:, :, None] == key_tiles[None, None, :]) & live_slots[:, :, None]
        return jnp.any(matches, axis=1)

    kv_blocks = [(0, stacked)]
    kv_blocks.append((-REACH + 2 * REACH * core, fifth_neighbour(stacked, chips)))
    fetched = []
    for chip_step in (1, 2):
        for sign in (1, -1):
            block = shifted(stacked, "chip", sign * chip_step)
            fetched.append((-sign * 2 * chip_step, block))
            kv_blocks.append((-sign * 2 * chip_step, block))
    own_late, _ = lax.optimization_barrier((stacked, fetched[0][1]))
    kv_blocks.append((1 - 2 * core, swapped(own_late, "core")))
    for offset, block in fetched:
        passed = swapped(block, "core")
        kv_blocks.append((offset + 1 - 2 * core, passed))

    tile_masks = jnp.stack([tile_need(offset) for offset, _ in kv_blocks]).astype(jnp.int32)
    attended = block_attention(queries, [b for _, b in kv_blocks], tile_masks.reshape(-1))
    weight_rows = lax.all_gather(out_weight, SEQ, axis=1, tiled=True)
    heads = lax.axis_size("head")
    if heads == 2:
        half = weight_rows.shape[1] // 2
        me = lax.axis_index("head")
        mine = lax.dynamic_slice_in_dim(weight_rows, me * half, half, 1)
        theirs = lax.dynamic_slice_in_dim(weight_rows, (1 - me) * half, half, 1)
        sent = jnp.dot(attended, theirs, preferred_element_type=jnp.float32).astype(jnp.bfloat16)
        got = swapped(sent, "head")
        kept_part = jnp.dot(attended, mine, preferred_element_type=jnp.float32).astype(jnp.bfloat16)
        kept_part = lax.optimization_barrier(kept_part)
        return (kept_part.astype(jnp.float32) + got.astype(jnp.float32)).astype(jnp.bfloat16)
    projected = jnp.dot(attended, weight_rows, preferred_element_type=jnp.float32)
    return lax.psum_scatter(projected.astype(jnp.bfloat16), "head", scatter_dimension=1, tiled=True)


def solution(mesh):
    heads = mesh.shape["head"]
    seq = mesh.shape["seq"]
    view = Mesh(mesh.devices.reshape(heads, seq // 2, 2), ("head", "chip", "core"))
    return jax.shard_map(
        local,
        mesh=view,
        in_specs=(P(SEQ, "head"), P(SEQ, "head"), P(SEQ, "head"), P("head", SEQ), P(), P()),
        out_specs=P(SEQ, "head"),
        check_vma=False,
    )
```

```python
import functools
import math

import jax
import jax.numpy as jnp
from jax import lax
from jax.experimental import pallas as pl
from jax.experimental.pallas import tpu as pltpu
from jax.sharding import Mesh
from jax.sharding import PartitionSpec as P

HD = 128
TILE = 128
REACH = 5

SEQ = ("chip", "core")

masked_floor = -1e30


def shifted(x, axis, by):
    peers = lax.axis_size(axis)
    pairs = [(i, i + by) for i in range(peers) if 0 <= i + by < peers]
    return lax.ppermute(x, axis, pairs)


def swapped(x, axis):
    return lax.ppermute(x, axis, [(0, 1), (1, 0)])


def third_neighbour(x, chips):
    peers = chips * 2
    pairs = []
    for s in range(peers):
        t = s + 3 if s % 2 == 1 else s - 3
        if 0 <= t < peers:
            pairs.append((s, t))
    return lax.ppermute(x, SEQ, pairs)


def attention_kernel(n_blocks, tiles, group, mask_ref, q_ref, *refs):
    kv_refs = refs[:n_blocks]
    out_ref = refs[n_blocks]
    score_ref = refs[n_blocks + 1]
    rows = q_ref.shape[0]
    for g in range(group):
        cols = slice(g * HD, (g + 1) * HD)
        query = q_ref[:, cols]
        for b in range(n_blocks):
            keys = kv_refs[b][0, :, cols]
            scores = lax.dot_general(
                query, keys, (((1,), (1,)), ((), ())), preferred_element_type=jnp.float32
            ) * (1.0 / math.sqrt(HD))
            for qi in range(tiles):
                for kt in range(tiles):
                    flag = mask_ref[(b * tiles + qi) * tiles + kt]
                    tile = scores[qi * TILE:(qi + 1) * TILE, kt * TILE:(kt + 1) * TILE]
                    score_ref[qi * TILE:(qi + 1) * TILE, b * rows + kt * TILE:b * rows + (kt + 1) * TILE] = (
                        jnp.where(flag != 0, tile, masked_floor)
                    )

        scores = score_ref[...]
        peak = jnp.max(scores, axis=1, keepdims=True)
        weights = jnp.exp(scores - peak)
        totals = jnp.sum(weights, axis=1, keepdims=True)
        rounded = weights.astype(jnp.bfloat16)
        summed = jnp.zeros((rows, HD), jnp.float32)
        for b in range(n_blocks):
            summed = summed + jnp.dot(
                rounded[:, b * rows:(b + 1) * rows], kv_refs[b][1, :, cols], preferred_element_type=jnp.float32
            )
        out_ref[:, cols] = (summed / totals).astype(out_ref.dtype)


def block_attention(queries, kv_list, flat_masks):
    rows, width = queries.shape
    heads = width // HD
    group = 5 if heads % 5 == 0 else 1
    n_blocks = len(kv_list)
    tiles = rows // TILE
    span = group * HD
    kv_spec = pl.BlockSpec((2, rows, span), lambda h, m: (0, 0, h))
    grid_spec = pltpu.PrefetchScalarGridSpec(
        num_scalar_prefetch=1,
        grid=(heads // group,),
        in_specs=[pl.BlockSpec((rows, span), lambda h, m: (0, h))] + [kv_spec] * n_blocks,
        out_specs=pl.BlockSpec((rows, span), lambda h, m: (0, h)),
        scratch_shapes=[pltpu.VMEM((rows, n_blocks * rows), jnp.float32)],
    )
    flops = 4 * rows * n_blocks * rows * HD * heads
    bytes_moved = 2 * (rows * width * 2 + n_blocks * 2 * rows * width)
    return pl.pallas_call(
        functools.partial(attention_kernel, n_blocks, tiles, group),
        grid_spec=grid_spec,
        out_shape=jax.ShapeDtypeStruct((rows, width), jnp.bfloat16),
        cost_estimate=pl.CostEstimate(
            flops=flops, transcendentals=rows * n_blocks * rows * heads, bytes_accessed=bytes_moved
        ),
    )(flat_masks, queries, *kv_list)


def local(queries, keys, values, out_weight, tile_lists, tile_counts):
    tok_rows, feat_width = queries.shape
    tiles_here = tok_rows // TILE
    heads_here = feat_width // HD
    chips = lax.axis_size("chip")
    core = lax.axis_index("core")
    device_index = lax.axis_index("chip") * 2 + core
    query_heads = queries.reshape(tok_rows, heads_here, HD)
    stacked = jnp.stack([keys, values])
    own_lists = lax.dynamic_slice_in_dim(tile_lists, device_index * tiles_here, tiles_here, 0)
    own_counts = lax.dynamic_slice_in_dim(tile_counts, device_index * tiles_here, tiles_here, 0)
    live_slots = jnp.arange(own_lists.shape[1], dtype=jnp.int32)[None, :] < own_counts[:, None]

    def tile_need(offset):
        key_tiles = (device_index + offset) * tiles_here + jnp.arange(tiles_here, dtype=jnp.int32)
        matches = (own_lists[:, :, None] == key_tiles[None, None, :]) & live_slots[:, :, None]
        return jnp.any(matches, axis=1)

    kv_blocks = [(0, stacked)]
    sibling = swapped(stacked, "core")
    kv_blocks.append((1 - 2 * core, sibling))
    fetched = []
    for chip_step in (1, 2):
        for sign in (1, -1):
            block = shifted(stacked, "chip", sign * chip_step)
            fetched.append((-sign * 2 * chip_step, block))
            kv_blocks.append((-sign * 2 * chip_step, block))
    from_below, from_above = fetched[0][1], fetched[1][1]
    onward = jnp.where(core == 1, from_below, from_above)
    kv_blocks.append((-REACH + 2 * REACH * core, third_neighbour(onward, chips)))
    for offset, block in fetched:
        passed = swapped(block, "core")
        kv_blocks.append((offset + 1 - 2 * core, passed))

    tile_masks = jnp.stack([tile_need(offset) for offset, _ in kv_blocks]).astype(jnp.int32)
    attended = block_attention(queries, [b for _, b in kv_blocks], tile_masks.reshape(-1))
    weight_rows = lax.all_gather(out_weight, SEQ, axis=1, tiled=True)
    heads = lax.axis_size("head")
    if heads == 2:
        half = weight_rows.shape[1] // 2
        me = lax.axis_index("head")
        mine = lax.dynamic_slice_in_dim(weight_rows, me * half, half, 1)
        theirs = lax.dynamic_slice_in_dim(weight_rows, (1 - me) * half, half, 1)
        sent = jnp.dot(attended, theirs, preferred_element_type=jnp.float32).astype(jnp.bfloat16)
        got = swapped(sent, "head")
        kept_part = jnp.dot(attended, mine, preferred_element_type=jnp.float32).astype(jnp.bfloat16)
        kept_part = lax.optimization_barrier(kept_part)
        return (kept_part.astype(jnp.float32) + got.astype(jnp.float32)).astype(jnp.bfloat16)
    projected = jnp.dot(attended, weight_rows, preferred_element_type=jnp.float32)
    return lax.psum_scatter(projected.astype(jnp.bfloat16), "head", scatter_dimension=1, tiled=True)


def solution(mesh):
    heads = mesh.shape["head"]
    seq = mesh.shape["seq"]
    view = Mesh(mesh.devices.reshape(heads, seq // 2, 2), ("head", "chip", "core"))
    return jax.shard_map(
        local,
        mesh=view,
        in_specs=(P(SEQ, "head"), P(SEQ, "head"), P(SEQ, "head"), P("head", SEQ), P(), P()),
        out_specs=P(SEQ, "head"),
        check_vma=False,
    )
```

```python
import functools
import math

import jax
import jax.numpy as jnp
from jax import lax
from jax.experimental import pallas as pl
from jax.experimental.pallas import tpu as pltpu
from jax.sharding import Mesh
from jax.sharding import PartitionSpec as P

HD = 128
TILE = 128
REACH = 5

SEQ = ("chip", "core")

masked_floor = -1e30


def shifted(x, axis, by):
    peers = lax.axis_size(axis)
    pairs = [(i, i + by) for i in range(peers) if 0 <= i + by < peers]
    return lax.ppermute(x, axis, pairs)


def swapped(x, axis):
    return lax.ppermute(x, axis, [(0, 1), (1, 0)])


def third_neighbour(x, chips):
    peers = chips * 2
    pairs = []
    for s in range(peers):
        t = s + 3 if s % 2 == 1 else s - 3
        if 0 <= t < peers:
            pairs.append((s, t))
    return lax.ppermute(x, SEQ, pairs)


def attention_kernel(n_blocks, tiles, group, carry_in, finish, mask_ref, q_ref, *refs):
    kv_refs = refs[:n_blocks]
    at = n_blocks
    if carry_in:
        acc_in, peak_in, total_in = refs[at:at + 3]
        at += 3
    if finish:
        out_ref = refs[at]
        at += 1
    else:
        acc_out, peak_out, total_out = refs[at:at + 3]
        at += 3
    score_ref = refs[at]
    rows = q_ref.shape[0]
    for g in range(group):
        cols = slice(g * HD, (g + 1) * HD)
        query = q_ref[:, cols]
        for b in range(n_blocks):
            keys = kv_refs[b][0, :, cols]
            scores = lax.dot_general(
                query, keys, (((1,), (1,)), ((), ())), preferred_element_type=jnp.float32
            ) * (1.0 / math.sqrt(HD))
            for qi in range(tiles):
                for kt in range(tiles):
                    flag = mask_ref[(b * tiles + qi) * tiles + kt]
                    tile = scores[qi * TILE:(qi + 1) * TILE, kt * TILE:(kt + 1) * TILE]
                    score_ref[qi * TILE:(qi + 1) * TILE, b * rows + kt * TILE:b * rows + (kt + 1) * TILE] = (
                        jnp.where(flag != 0, tile, masked_floor)
                    )

        scores = score_ref[...]
        peak = jnp.max(scores, axis=1, keepdims=True)
        if carry_in:
            old_peak = peak_in[:, g * HD:g * HD + 1]
            peak = jnp.maximum(peak, old_peak)
            carried = jnp.exp(old_peak - peak)
        weights = jnp.exp(scores - peak)
        totals = jnp.sum(weights, axis=1, keepdims=True)
        rounded = weights.astype(jnp.bfloat16)
        summed = jnp.zeros((rows, HD), jnp.float32)
        for b in range(n_blocks):
            summed = summed + jnp.dot(
                rounded[:, b * rows:(b + 1) * rows], kv_refs[b][1, :, cols], preferred_element_type=jnp.float32
            )
        if carry_in:
            totals = carried * total_in[:, g * HD:g * HD + 1] + totals
            summed = carried * acc_in[:, cols] + summed
        if finish:
            out_ref[:, cols] = (summed / totals).astype(out_ref.dtype)
        else:
            acc_out[:, cols] = summed
            peak_out[:, cols] = jnp.broadcast_to(peak, (rows, HD))
            total_out[:, cols] = jnp.broadcast_to(totals, (rows, HD))


def block_attention(queries, kv_list, flat_masks, carry=None, finish=True):
    rows, width = queries.shape
    heads = width // HD
    group = 5 if heads % 5 == 0 else 1
    n_blocks = len(kv_list)
    tiles = rows // TILE
    span = group * HD
    kv_spec = pl.BlockSpec((2, rows, span), lambda h, m: (0, 0, h))
    row_spec = pl.BlockSpec((rows, span), lambda h, m: (0, h))
    state_shape = jax.ShapeDtypeStruct((rows, width), jnp.float32)
    in_specs = [row_spec] + [kv_spec] * n_blocks
    operands = [flat_masks, queries, *kv_list]
    if carry is not None:
        in_specs += [row_spec] * 3
        operands += list(carry)
    if finish:
        out_shape = jax.ShapeDtypeStruct((rows, width), jnp.bfloat16)
        out_specs = row_spec
    else:
        out_shape = (state_shape,) * 3
        out_specs = (row_spec,) * 3
    grid_spec = pltpu.PrefetchScalarGridSpec(
        num_scalar_prefetch=1,
        grid=(heads // group,),
        in_specs=in_specs,
        out_specs=out_specs,
        scratch_shapes=[pltpu.VMEM((rows, n_blocks * rows), jnp.float32)],
    )
    flops = 4 * rows * n_blocks * rows * HD * heads
    bytes_moved = 2 * (rows * width * 2 + n_blocks * 2 * rows * width) + 24 * rows * width
    return pl.pallas_call(
        functools.partial(attention_kernel, n_blocks, tiles, group, carry is not None, finish),
        grid_spec=grid_spec,
        out_shape=out_shape,
        cost_estimate=pl.CostEstimate(
            flops=flops, transcendentals=rows * n_blocks * rows * heads, bytes_accessed=bytes_moved
        ),
    )(*operands)


def local(queries, keys, values, out_weight, tile_lists, tile_counts):
    tok_rows, feat_width = queries.shape
    tiles_here = tok_rows // TILE
    heads_here = feat_width // HD
    chips = lax.axis_size("chip")
    core = lax.axis_index("core")
    device_index = lax.axis_index("chip") * 2 + core
    query_heads = queries.reshape(tok_rows, heads_here, HD)
    stacked = jnp.stack([keys, values])
    own_lists = lax.dynamic_slice_in_dim(tile_lists, device_index * tiles_here, tiles_here, 0)
    own_counts = lax.dynamic_slice_in_dim(tile_counts, device_index * tiles_here, tiles_here, 0)
    live_slots = jnp.arange(own_lists.shape[1], dtype=jnp.int32)[None, :] < own_counts[:, None]

    def tile_need(offset):
        key_tiles = (device_index + offset) * tiles_here + jnp.arange(tiles_here, dtype=jnp.int32)
        matches = (own_lists[:, :, None] == key_tiles[None, None, :]) & live_slots[:, :, None]
        return jnp.any(matches, axis=1)

    early = [(0, stacked)]
    sibling = swapped(stacked, "core")
    early.append((1 - 2 * core, sibling))
    fetched = []
    for chip_step in (1, 2):
        for sign in (1, -1):
            block = shifted(stacked, "chip", sign * chip_step)
            fetched.append((-sign * 2 * chip_step, block))
            early.append((-sign * 2 * chip_step, block))
    from_below, from_above = fetched[0][1], fetched[1][1]
    onward = jnp.where(core == 1, from_below, from_above)
    late = [(-REACH + 2 * REACH * core, third_neighbour(onward, chips))]
    for offset, block in fetched:
        passed = swapped(block, "core")
        late.append((offset + 1 - 2 * core, passed))

    def masks_of(blocks):
        return jnp.stack([tile_need(offset) for offset, _ in blocks]).astype(jnp.int32).reshape(-1)

    carry = block_attention(queries, [b for _, b in early], masks_of(early), finish=False)
    attended = block_attention(queries, [b for _, b in late], masks_of(late), carry=carry)
    weight_rows = lax.all_gather(out_weight, SEQ, axis=1, tiled=True)
    heads = lax.axis_size("head")
    if heads == 2:
        half = weight_rows.shape[1] // 2
        me = lax.axis_index("head")
        mine = lax.dynamic_slice_in_dim(weight_rows, me * half, half, 1)
        theirs = lax.dynamic_slice_in_dim(weight_rows, (1 - me) * half, half, 1)
        sent = jnp.dot(attended, theirs, preferred_element_type=jnp.float32).astype(jnp.bfloat16)
        got = swapped(sent, "head")
        kept_part = jnp.dot(attended, mine, preferred_element_type=jnp.float32).astype(jnp.bfloat16)
        kept_part = lax.optimization_barrier(kept_part)
        return (kept_part.astype(jnp.float32) + got.astype(jnp.float32)).astype(jnp.bfloat16)
    projected = jnp.dot(attended, weight_rows, preferred_element_type=jnp.float32)
    return lax.psum_scatter(projected.astype(jnp.bfloat16), "head", scatter_dimension=1, tiled=True)


def solution(mesh):
    heads = mesh.shape["head"]
    seq = mesh.shape["seq"]
    view = Mesh(mesh.devices.reshape(heads, seq // 2, 2), ("head", "chip", "core"))
    return jax.shard_map(
        local,
        mesh=view,
        in_specs=(P(SEQ, "head"), P(SEQ, "head"), P(SEQ, "head"), P("head", SEQ), P(), P()),
        out_specs=P(SEQ, "head"),
        check_vma=False,
    )
```

```python
import functools
import math

import jax
import jax.numpy as jnp
from jax import lax
from jax.experimental import pallas as pl
from jax.experimental.pallas import tpu as pltpu
from jax.sharding import Mesh
from jax.sharding import PartitionSpec as P

HD = 128
TILE = 128
REACH = 5

SEQ = ("chip", "core")

masked_floor = -1e30


def shifted(x, axis, by):
    peers = lax.axis_size(axis)
    pairs = [(i, i + by) for i in range(peers) if 0 <= i + by < peers]
    return lax.ppermute(x, axis, pairs)


def swapped(x, axis):
    return lax.ppermute(x, axis, [(0, 1), (1, 0)])


def third_neighbour(x, chips):
    peers = chips * 2
    pairs = []
    for s in range(peers):
        t = s + 3 if s % 2 == 1 else s - 3
        if 0 <= t < peers:
            pairs.append((s, t))
    return lax.ppermute(x, SEQ, pairs)


def attention_kernel(n_blocks, q_tiles, k_tiles, group, carry_in, finish, mask_ref, q_ref, *refs):
    kv_refs = refs[:n_blocks]
    at = n_blocks
    if carry_in:
        acc_in, peak_in, total_in = refs[at:at + 3]
        at += 3
    if finish:
        out_ref = refs[at]
        at += 1
    else:
        acc_out, peak_out, total_out = refs[at:at + 3]
        at += 3
    score_ref = refs[at]
    rows = q_ref.shape[0]
    k_rows = k_tiles * TILE
    for g in range(group):
        cols = slice(g * HD, (g + 1) * HD)
        query = q_ref[:, cols]
        for b in range(n_blocks):
            keys = kv_refs[b][0, :, cols]
            scores = lax.dot_general(
                query, keys, (((1,), (1,)), ((), ())), preferred_element_type=jnp.float32
            ) * (1.0 / math.sqrt(HD))
            for qi in range(q_tiles):
                for kt in range(k_tiles):
                    flag = mask_ref[(b * q_tiles + qi) * k_tiles + kt]
                    tile = scores[qi * TILE:(qi + 1) * TILE, kt * TILE:(kt + 1) * TILE]
                    score_ref[qi * TILE:(qi + 1) * TILE, b * k_rows + kt * TILE:b * k_rows + (kt + 1) * TILE] = (
                        jnp.where(flag != 0, tile, masked_floor)
                    )

        scores = score_ref[...]
        peak = jnp.max(scores, axis=1, keepdims=True)
        if carry_in:
            old_peak = peak_in[:, g * HD:g * HD + 1]
            peak = jnp.maximum(peak, old_peak)
            carried = jnp.exp(old_peak - peak)
        weights = jnp.exp(scores - peak)
        totals = jnp.sum(weights, axis=1, keepdims=True)
        rounded = weights.astype(jnp.bfloat16)
        summed = jnp.zeros((rows, HD), jnp.float32)
        for b in range(n_blocks):
            summed = summed + jnp.dot(
                rounded[:, b * k_rows:(b + 1) * k_rows], kv_refs[b][1, :, cols], preferred_element_type=jnp.float32
            )
        if carry_in:
            totals = carried * total_in[:, g * HD:g * HD + 1] + totals
            summed = carried * acc_in[:, cols] + summed
        if finish:
            out_ref[:, cols] = (summed / totals).astype(out_ref.dtype)
        else:
            acc_out[:, cols] = summed
            peak_out[:, cols] = jnp.broadcast_to(peak, (rows, HD))
            total_out[:, cols] = jnp.broadcast_to(totals, (rows, HD))


def block_attention(queries, kv_list, flat_masks, carry=None, finish=True):
    rows, width = queries.shape
    k_rows = kv_list[0].shape[1]
    heads = width // HD
    group = 5 if heads % 5 == 0 else 1
    n_blocks = len(kv_list)
    span = group * HD
    kv_spec = pl.BlockSpec((2, k_rows, span), lambda h, m: (0, 0, h))
    row_spec = pl.BlockSpec((rows, span), lambda h, m: (0, h))
    state_shape = jax.ShapeDtypeStruct((rows, width), jnp.float32)
    in_specs = [row_spec] + [kv_spec] * n_blocks
    operands = [flat_masks, queries, *kv_list]
    if carry is not None:
        in_specs += [row_spec] * 3
        operands += list(carry)
    if finish:
        out_shape = jax.ShapeDtypeStruct((rows, width), jnp.bfloat16)
        out_specs = row_spec
    else:
        out_shape = (state_shape,) * 3
        out_specs = (row_spec,) * 3
    grid_spec = pltpu.PrefetchScalarGridSpec(
        num_scalar_prefetch=1,
        grid=(heads // group,),
        in_specs=in_specs,
        out_specs=out_specs,
        scratch_shapes=[pltpu.VMEM((rows, n_blocks * k_rows), jnp.float32)],
    )
    flops = 4 * rows * n_blocks * k_rows * HD * heads
    bytes_moved = 2 * (rows * width + n_blocks * 2 * k_rows * width) + 24 * rows * width
    return pl.pallas_call(
        functools.partial(attention_kernel, n_blocks, rows // TILE, k_rows // TILE, group, carry is not None, finish),
        grid_spec=grid_spec,
        out_shape=out_shape,
        cost_estimate=pl.CostEstimate(
            flops=flops, transcendentals=rows * n_blocks * k_rows * heads, bytes_accessed=bytes_moved
        ),
    )(*operands)


def local(queries, keys, values, out_weight, tile_lists, tile_counts):
    tok_rows, feat_width = queries.shape
    tiles_here = tok_rows // TILE
    heads_here = feat_width // HD
    chips = lax.axis_size("chip")
    core = lax.axis_index("core")
    device_index = lax.axis_index("chip") * 2 + core
    query_heads = queries.reshape(tok_rows, heads_here, HD)
    stacked = jnp.stack([keys, values])
    own_lists = lax.dynamic_slice_in_dim(tile_lists, device_index * tiles_here, tiles_here, 0)
    own_counts = lax.dynamic_slice_in_dim(tile_counts, device_index * tiles_here, tiles_here, 0)
    live_slots = jnp.arange(own_lists.shape[1], dtype=jnp.int32)[None, :] < own_counts[:, None]

    def tile_need(offset):
        key_tiles = (device_index + offset) * tiles_here + jnp.arange(tiles_here, dtype=jnp.int32)
        matches = (own_lists[:, :, None] == key_tiles[None, None, :]) & live_slots[:, :, None]
        return jnp.any(matches, axis=1)

    early = [(0, stacked)]
    sibling = swapped(stacked, "core")
    early.append((1 - 2 * core, sibling))
    fetched = []
    for chip_step in (1, 2):
        for sign in (1, -1):
            block = shifted(stacked, "chip", sign * chip_step)
            fetched.append((-sign * 2 * chip_step, block))
            early.append((-sign * 2 * chip_step, block))
    from_below, from_above = fetched[0][1], fetched[1][1]
    onward = jnp.where(core == 1, from_below, from_above)
    late = [(-REACH + 2 * REACH * core, third_neighbour(onward, chips))]
    for offset, block in fetched:
        passed = swapped(block, "core")
        late.append((offset + 1 - 2 * core, passed))

    def masks_of(blocks, q_tile=None):
        need = jnp.stack([tile_need(offset) for offset, _ in blocks]).astype(jnp.int32)
        if q_tile is not None:
            need = need[:, q_tile:q_tile + 1, :]
        return need.reshape(-1)

    carry = block_attention(queries, [b for _, b in early], masks_of(early), finish=False)
    weight_rows = lax.all_gather(out_weight, SEQ, axis=1, tiled=True)
    heads = lax.axis_size("head")
    if heads != 2:
        attended = block_attention(queries, [b for _, b in late], masks_of(late), carry=carry)
        projected = jnp.dot(attended, weight_rows, preferred_element_type=jnp.float32)
        return lax.psum_scatter(projected.astype(jnp.bfloat16), "head", scatter_dimension=1, tiled=True)
    half = weight_rows.shape[1] // 2
    me = lax.axis_index("head")
    mine = lax.dynamic_slice_in_dim(weight_rows, me * half, half, 1)
    theirs = lax.dynamic_slice_in_dim(weight_rows, (1 - me) * half, half, 1)
    pieces = []
    for q_tile in range(tiles_here):
        rows = slice(q_tile * TILE, (q_tile + 1) * TILE)
        attended = block_attention(
            queries[rows], [b for _, b in late], masks_of(late, q_tile), carry=[c[rows] for c in carry]
        )
        sent = jnp.dot(attended, theirs, preferred_element_type=jnp.float32).astype(jnp.bfloat16)
        got = swapped(sent, "head")
        kept_part = jnp.dot(attended, mine, preferred_element_type=jnp.float32).astype(jnp.bfloat16)
        kept_part = lax.optimization_barrier(kept_part)
        pieces.append((kept_part.astype(jnp.float32) + got.astype(jnp.float32)).astype(jnp.bfloat16))
    return jnp.concatenate(pieces, axis=0)


def solution(mesh):
    heads = mesh.shape["head"]
    seq = mesh.shape["seq"]
    view = Mesh(mesh.devices.reshape(heads, seq // 2, 2), ("head", "chip", "core"))
    return jax.shard_map(
        local,
        mesh=view,
        in_specs=(P(SEQ, "head"), P(SEQ, "head"), P(SEQ, "head"), P("head", SEQ), P(), P()),
        out_specs=P(SEQ, "head"),
        check_vma=False,
    )
```

```python
import functools
import math

import jax
import jax.numpy as jnp
from jax import lax
from jax.experimental import pallas as pl
from jax.experimental.pallas import tpu as pltpu
from jax.sharding import Mesh
from jax.sharding import PartitionSpec as P

HD = 128
TILE = 128
REACH = 5

SEQ = ("chip", "core")

masked_floor = -1e30


def shifted(x, axis, by):
    peers = lax.axis_size(axis)
    pairs = [(i, i + by) for i in range(peers) if 0 <= i + by < peers]
    return lax.ppermute(x, axis, pairs)


def swapped(x, axis):
    return lax.ppermute(x, axis, [(0, 1), (1, 0)])


def third_neighbour(x, chips):
    peers = chips * 2
    pairs = []
    for s in range(peers):
        t = s + 3 if s % 2 == 1 else s - 3
        if 0 <= t < peers:
            pairs.append((s, t))
    return lax.ppermute(x, SEQ, pairs)


def attention_kernel(n_blocks, tiles, group, carry_in, finish, mask_ref, q_ref, *refs):
    kv_refs = refs[:n_blocks]
    at = n_blocks
    if carry_in:
        acc_in, peak_in, total_in = refs[at:at + 3]
        at += 3
    if finish:
        out_ref = refs[at]
        at += 1
    else:
        acc_out, peak_out, total_out = refs[at:at + 3]
        at += 3
    score_ref = refs[at]
    rows = q_ref.shape[0]
    for g in range(group):
        cols = slice(g * HD, (g + 1) * HD)
        query = q_ref[:, cols]
        for b in range(n_blocks):
            keys = kv_refs[b][0, :, cols]
            scores = lax.dot_general(
                query, keys, (((1,), (1,)), ((), ())), preferred_element_type=jnp.float32
            ) * (1.0 / math.sqrt(HD))
            for qi in range(tiles):
                for kt in range(tiles):
                    flag = mask_ref[(b * tiles + qi) * tiles + kt]
                    tile = scores[qi * TILE:(qi + 1) * TILE, kt * TILE:(kt + 1) * TILE]
                    score_ref[qi * TILE:(qi + 1) * TILE, b * rows + kt * TILE:b * rows + (kt + 1) * TILE] = (
                        jnp.where(flag != 0, tile, masked_floor)
                    )

        scores = score_ref[...]
        peak = jnp.max(scores, axis=1, keepdims=True)
        if carry_in:
            old_peak = peak_in[:, g * HD:g * HD + 1]
            peak = jnp.maximum(peak, old_peak)
            carried = jnp.exp(old_peak - peak)
        weights = jnp.exp(scores - peak)
        totals = jnp.sum(weights, axis=1, keepdims=True)
        rounded = weights.astype(jnp.bfloat16)
        summed = jnp.zeros((rows, HD), jnp.float32)
        for b in range(n_blocks):
            summed = summed + jnp.dot(
                rounded[:, b * rows:(b + 1) * rows], kv_refs[b][1, :, cols], preferred_element_type=jnp.float32
            )
        if carry_in:
            totals = carried * total_in[:, g * HD:g * HD + 1] + totals
            summed = carried * acc_in[:, cols] + summed
        if finish:
            out_ref[:, cols] = (summed / totals).astype(out_ref.dtype)
        else:
            acc_out[:, cols] = summed
            peak_out[:, cols] = jnp.broadcast_to(peak, (rows, HD))
            total_out[:, cols] = jnp.broadcast_to(totals, (rows, HD))


def block_attention(queries, kv_list, flat_masks, carry=None, finish=True):
    rows, width = queries.shape
    heads = width // HD
    group = 5 if heads % 5 == 0 else 1
    n_blocks = len(kv_list)
    tiles = rows // TILE
    span = group * HD
    kv_spec = pl.BlockSpec((2, rows, span), lambda h, m: (0, 0, h))
    row_spec = pl.BlockSpec((rows, span), lambda h, m: (0, h))
    state_shape = jax.ShapeDtypeStruct((rows, width), jnp.float32)
    in_specs = [row_spec] + [kv_spec] * n_blocks
    operands = [flat_masks, queries, *kv_list]
    if carry is not None:
        in_specs += [row_spec] * 3
        operands += list(carry)
    if finish:
        out_shape = jax.ShapeDtypeStruct((rows, width), jnp.bfloat16)
        out_specs = row_spec
    else:
        out_shape = (state_shape,) * 3
        out_specs = (row_spec,) * 3
    grid_spec = pltpu.PrefetchScalarGridSpec(
        num_scalar_prefetch=1,
        grid=(heads // group,),
        in_specs=in_specs,
        out_specs=out_specs,
        scratch_shapes=[pltpu.VMEM((rows, n_blocks * rows), jnp.float32)],
    )
    flops = 4 * rows * n_blocks * rows * HD * heads
    bytes_moved = 2 * (rows * width * 2 + n_blocks * 2 * rows * width) + 24 * rows * width
    return pl.pallas_call(
        functools.partial(attention_kernel, n_blocks, tiles, group, carry is not None, finish),
        grid_spec=grid_spec,
        out_shape=out_shape,
        cost_estimate=pl.CostEstimate(
            flops=flops, transcendentals=rows * n_blocks * rows * heads, bytes_accessed=bytes_moved
        ),
    )(*operands)


def local(queries, keys, values, out_weight, tile_lists, tile_counts):
    tok_rows, feat_width = queries.shape
    tiles_here = tok_rows // TILE
    heads_here = feat_width // HD
    chips = lax.axis_size("chip")
    core = lax.axis_index("core")
    device_index = lax.axis_index("chip") * 2 + core
    query_heads = queries.reshape(tok_rows, heads_here, HD)
    stacked = jnp.stack([keys, values])
    own_lists = lax.dynamic_slice_in_dim(tile_lists, device_index * tiles_here, tiles_here, 0)
    own_counts = lax.dynamic_slice_in_dim(tile_counts, device_index * tiles_here, tiles_here, 0)
    live_slots = jnp.arange(own_lists.shape[1], dtype=jnp.int32)[None, :] < own_counts[:, None]

    def tile_need(offset):
        key_tiles = (device_index + offset) * tiles_here + jnp.arange(tiles_here, dtype=jnp.int32)
        matches = (own_lists[:, :, None] == key_tiles[None, None, :]) & live_slots[:, :, None]
        return jnp.any(matches, axis=1)

    early = [(0, stacked)]
    sibling = swapped(stacked, "core")
    early.append((1 - 2 * core, sibling))
    fetched = []
    for chip_step in (1, 2):
        for sign in (1, -1):
            block = shifted(stacked, "chip", sign * chip_step)
            fetched.append((-sign * 2 * chip_step, block))
            early.append((-sign * 2 * chip_step, block))
    from_below, from_above = fetched[0][1], fetched[1][1]
    onward = jnp.where(core == 1, from_below, from_above)
    late = [(-REACH + 2 * REACH * core, third_neighbour(onward, chips))]
    for offset, block in fetched:
        passed = swapped(block, "core")
        late.append((offset + 1 - 2 * core, passed))

    def masks_of(blocks):
        return jnp.stack([tile_need(offset) for offset, _ in blocks]).astype(jnp.int32).reshape(-1)

    carry = block_attention(queries, [b for _, b in early], masks_of(early), finish=False)
    attended = block_attention(queries, [b for _, b in late], masks_of(late), carry=carry)
    weight_rows = lax.all_gather(out_weight, SEQ, axis=1, tiled=True)
    heads = lax.axis_size("head")
    if heads == 2:
        half = weight_rows.shape[1] // 2
        me = lax.axis_index("head")
        mine = lax.dynamic_slice_in_dim(weight_rows, me * half, half, 1)
        theirs = lax.dynamic_slice_in_dim(weight_rows, (1 - me) * half, half, 1)
        chunk = half // 2
        got = []
        for part in range(2):
            cols = slice(part * chunk, (part + 1) * chunk)
            sent = jnp.dot(attended, theirs[:, cols], preferred_element_type=jnp.float32).astype(jnp.bfloat16)
            got.append(swapped(sent, "head"))
        kept_part = jnp.dot(attended, mine, preferred_element_type=jnp.float32).astype(jnp.bfloat16)
        kept_part = lax.optimization_barrier(kept_part)
        got = jnp.concatenate(got, axis=1)
        return (kept_part.astype(jnp.float32) + got.astype(jnp.float32)).astype(jnp.bfloat16)
    projected = jnp.dot(attended, weight_rows, preferred_element_type=jnp.float32)
    return lax.psum_scatter(projected.astype(jnp.bfloat16), "head", scatter_dimension=1, tiled=True)


def solution(mesh):
    heads = mesh.shape["head"]
    seq = mesh.shape["seq"]
    view = Mesh(mesh.devices.reshape(heads, seq // 2, 2), ("head", "chip", "core"))
    return jax.shard_map(
        local,
        mesh=view,
        in_specs=(P(SEQ, "head"), P(SEQ, "head"), P(SEQ, "head"), P("head", SEQ), P(), P()),
        out_specs=P(SEQ, "head"),
        check_vma=False,
    )
```

```python
import functools
import math

import jax
import jax.numpy as jnp
from jax import lax
from jax.experimental import pallas as pl
from jax.experimental.pallas import tpu as pltpu
from jax.sharding import Mesh
from jax.sharding import PartitionSpec as P

HD = 128
TILE = 128
REACH = 5

SEQ = ("chip", "core")

masked_floor = -1e30


def shifted(x, axis, by):
    peers = lax.axis_size(axis)
    pairs = [(i, i + by) for i in range(peers) if 0 <= i + by < peers]
    return lax.ppermute(x, axis, pairs)


def swapped(x, axis):
    return lax.ppermute(x, axis, [(0, 1), (1, 0)])


def third_neighbour(x, chips):
    peers = chips * 2
    pairs = []
    for s in range(peers):
        t = s + 3 if s % 2 == 1 else s - 3
        if 0 <= t < peers:
            pairs.append((s, t))
    return lax.ppermute(x, SEQ, pairs)


def attention_kernel(n_blocks, tiles, group, carry_in, finish, mask_ref, q_ref, *refs):
    kv_refs = refs[:n_blocks]
    at = n_blocks
    if carry_in:
        acc_in, peak_in, total_in = refs[at:at + 3]
        at += 3
    if finish:
        out_ref = refs[at]
        at += 1
    else:
        acc_out, peak_out, total_out = refs[at:at + 3]
        at += 3
    score_ref = refs[at]
    rows = q_ref.shape[0]
    for g in range(group):
        cols = slice(g * HD, (g + 1) * HD)
        query = q_ref[:, cols]
        for b in range(n_blocks):
            keys = kv_refs[b][0, :, cols]
            scores = lax.dot_general(
                query, keys, (((1,), (1,)), ((), ())), preferred_element_type=jnp.float32
            ) * (1.0 / math.sqrt(HD))
            for qi in range(tiles):
                for kt in range(tiles):
                    flag = mask_ref[(b * tiles + qi) * tiles + kt]
                    tile = scores[qi * TILE:(qi + 1) * TILE, kt * TILE:(kt + 1) * TILE]
                    score_ref[qi * TILE:(qi + 1) * TILE, b * rows + kt * TILE:b * rows + (kt + 1) * TILE] = (
                        jnp.where(flag != 0, tile, masked_floor)
                    )

        scores = score_ref[...]
        peak = jnp.max(scores, axis=1, keepdims=True)
        if carry_in:
            old_peak = peak_in[:, g * HD:g * HD + 1]
            peak = jnp.maximum(peak, old_peak)
            carried = jnp.exp(old_peak - peak)
        weights = jnp.exp(scores - peak)
        totals = jnp.sum(weights, axis=1, keepdims=True)
        rounded = weights.astype(jnp.bfloat16)
        summed = jnp.zeros((rows, HD), jnp.float32)
        for b in range(n_blocks):
            summed = summed + jnp.dot(
                rounded[:, b * rows:(b + 1) * rows], kv_refs[b][1, :, cols], preferred_element_type=jnp.float32
            )
        if carry_in:
            totals = carried * total_in[:, g * HD:g * HD + 1] + totals
            summed = carried * acc_in[:, cols] + summed
        if finish:
            out_ref[:, cols] = (summed / totals).astype(out_ref.dtype)
        else:
            acc_out[:, cols] = summed
            peak_out[:, cols] = jnp.broadcast_to(peak, (rows, HD))
            total_out[:, cols] = jnp.broadcast_to(totals, (rows, HD))


def block_attention(queries, kv_list, flat_masks, carry=None, finish=True):
    rows, width = queries.shape
    heads = width // HD
    group = 5 if heads % 5 == 0 else 1
    n_blocks = len(kv_list)
    tiles = rows // TILE
    span = group * HD
    kv_spec = pl.BlockSpec((2, rows, span), lambda h, m: (0, 0, h))
    row_spec = pl.BlockSpec((rows, span), lambda h, m: (0, h))
    state_shape = jax.ShapeDtypeStruct((rows, width), jnp.float32)
    in_specs = [row_spec] + [kv_spec] * n_blocks
    operands = [flat_masks, queries, *kv_list]
    if carry is not None:
        in_specs += [row_spec] * 3
        operands += list(carry)
    if finish:
        out_shape = jax.ShapeDtypeStruct((rows, width), jnp.bfloat16)
        out_specs = row_spec
    else:
        out_shape = (state_shape,) * 3
        out_specs = (row_spec,) * 3
    grid_spec = pltpu.PrefetchScalarGridSpec(
        num_scalar_prefetch=1,
        grid=(heads // group,),
        in_specs=in_specs,
        out_specs=out_specs,
        scratch_shapes=[pltpu.VMEM((rows, n_blocks * rows), jnp.float32)],
    )
    flops = 4 * rows * n_blocks * rows * HD * heads
    bytes_moved = 2 * (rows * width * 2 + n_blocks * 2 * rows * width) + 24 * rows * width
    return pl.pallas_call(
        functools.partial(attention_kernel, n_blocks, tiles, group, carry is not None, finish),
        grid_spec=grid_spec,
        out_shape=out_shape,
        cost_estimate=pl.CostEstimate(
            flops=flops, transcendentals=rows * n_blocks * rows * heads, bytes_accessed=bytes_moved
        ),
    )(*operands)


def local(queries, keys, values, out_weight, tile_lists, tile_counts):
    tok_rows, feat_width = queries.shape
    tiles_here = tok_rows // TILE
    heads_here = feat_width // HD
    chips = lax.axis_size("chip")
    core = lax.axis_index("core")
    device_index = lax.axis_index("chip") * 2 + core
    query_heads = queries.reshape(tok_rows, heads_here, HD)
    stacked = jnp.stack([keys, values])
    own_lists = lax.dynamic_slice_in_dim(tile_lists, device_index * tiles_here, tiles_here, 0)
    own_counts = lax.dynamic_slice_in_dim(tile_counts, device_index * tiles_here, tiles_here, 0)
    live_slots = jnp.arange(own_lists.shape[1], dtype=jnp.int32)[None, :] < own_counts[:, None]

    def tile_need(offset):
        key_tiles = (device_index + offset) * tiles_here + jnp.arange(tiles_here, dtype=jnp.int32)
        matches = (own_lists[:, :, None] == key_tiles[None, None, :]) & live_slots[:, :, None]
        return jnp.any(matches, axis=1)

    early = [(0, stacked)]
    sibling = swapped(stacked, "core")
    early.append((1 - 2 * core, sibling))
    fetched = []
    for chip_step in (1, 2):
        for sign in (1, -1):
            block = shifted(stacked, "chip", sign * chip_step)
            fetched.append((-sign * 2 * chip_step, block))
            early.append((-sign * 2 * chip_step, block))
    from_below, from_above = fetched[0][1], fetched[1][1]
    onward = jnp.where(core == 1, from_below, from_above)
    late = [(-REACH + 2 * REACH * core, third_neighbour(onward, chips))]
    for offset, block in fetched:
        passed = swapped(block, "core")
        late.append((offset + 1 - 2 * core, passed))

    def masks_of(blocks):
        return jnp.stack([tile_need(offset) for offset, _ in blocks]).astype(jnp.int32).reshape(-1)

    carry = block_attention(queries, [b for _, b in early], masks_of(early), finish=False)
    attended = block_attention(queries, [b for _, b in late], masks_of(late), carry=carry)
    weight_rows = lax.all_gather(out_weight, SEQ, axis=1, tiled=True)
    heads = lax.axis_size("head")
    if heads == 2:
        half = weight_rows.shape[1] // 2
        me = lax.axis_index("head")
        mine = lax.dynamic_slice_in_dim(weight_rows, me * half, half, 1)
        theirs = lax.dynamic_slice_in_dim(weight_rows, (1 - me) * half, half, 1)
        parts = 4
        chunk = half // parts
        got = []
        for part in range(parts):
            cols = slice(part * chunk, (part + 1) * chunk)
            sent = jnp.dot(attended, theirs[:, cols], preferred_element_type=jnp.float32).astype(jnp.bfloat16)
            got.append(swapped(sent, "head"))
        kept_part = jnp.dot(attended, mine, preferred_element_type=jnp.float32).astype(jnp.bfloat16)
        kept_part = lax.optimization_barrier(kept_part)
        got = jnp.concatenate(got, axis=1)
        return (kept_part.astype(jnp.float32) + got.astype(jnp.float32)).astype(jnp.bfloat16)
    projected = jnp.dot(attended, weight_rows, preferred_element_type=jnp.float32)
    return lax.psum_scatter(projected.astype(jnp.bfloat16), "head", scatter_dimension=1, tiled=True)


def solution(mesh):
    heads = mesh.shape["head"]
    seq = mesh.shape["seq"]
    view = Mesh(mesh.devices.reshape(heads, seq // 2, 2), ("head", "chip", "core"))
    return jax.shard_map(
        local,
        mesh=view,
        in_specs=(P(SEQ, "head"), P(SEQ, "head"), P(SEQ, "head"), P("head", SEQ), P(), P()),
        out_specs=P(SEQ, "head"),
        check_vma=False,
    )
```

```python
import functools
import math

import jax
import jax.numpy as jnp
from jax import lax
from jax.experimental import pallas as pl
from jax.experimental.pallas import tpu as pltpu
from jax.sharding import Mesh
from jax.sharding import PartitionSpec as P

HD = 128
TILE = 128
REACH = 5

SEQ = ("chip", "core")

masked_floor = -1e30


def shifted(x, axis, by):
    peers = lax.axis_size(axis)
    pairs = [(i, i + by) for i in range(peers) if 0 <= i + by < peers]
    return lax.ppermute(x, axis, pairs)


def swapped(x, axis):
    return lax.ppermute(x, axis, [(0, 1), (1, 0)])


def fifth_routes(onward, across, chips):
    far, near = [], []
    for c in range(chips):
        if c % 2 == 0:
            src = 2 * c + 1
            if c + 2 < chips:
                far.append((src, 2 * (c + 2)))
            if c + 1 < chips:
                near.append((src, 2 * (c + 1)))
        else:
            src = 2 * c
            if c - 2 >= 0:
                far.append((src, 2 * (c - 2) + 1))
            near.append((src, 2 * (c - 1) + 1))
    return lax.ppermute(onward, SEQ, far), lax.ppermute(across, SEQ, near)


def attention_kernel(n_blocks, tiles, group, carry_in, finish, mask_ref, q_ref, *refs):
    kv_refs = refs[:n_blocks]
    at = n_blocks
    if carry_in:
        acc_in, peak_in, total_in = refs[at:at + 3]
        at += 3
    if finish:
        out_ref = refs[at]
        at += 1
    else:
        acc_out, peak_out, total_out = refs[at:at + 3]
        at += 3
    score_ref = refs[at]
    rows = q_ref.shape[0]
    for g in range(group):
        cols = slice(g * HD, (g + 1) * HD)
        query = q_ref[:, cols]
        for b in range(n_blocks):
            keys = kv_refs[b][0, :, cols]
            scores = lax.dot_general(
                query, keys, (((1,), (1,)), ((), ())), preferred_element_type=jnp.float32
            ) * (1.0 / math.sqrt(HD))
            for qi in range(tiles):
                for kt in range(tiles):
                    flag = mask_ref[(b * tiles + qi) * tiles + kt]
                    tile = scores[qi * TILE:(qi + 1) * TILE, kt * TILE:(kt + 1) * TILE]
                    score_ref[qi * TILE:(qi + 1) * TILE, b * rows + kt * TILE:b * rows + (kt + 1) * TILE] = (
                        jnp.where(flag != 0, tile, masked_floor)
                    )

        scores = score_ref[...]
        peak = jnp.max(scores, axis=1, keepdims=True)
        if carry_in:
            old_peak = peak_in[:, g * HD:g * HD + 1]
            peak = jnp.maximum(peak, old_peak)
            carried = jnp.exp(old_peak - peak)
        weights = jnp.exp(scores - peak)
        totals = jnp.sum(weights, axis=1, keepdims=True)
        rounded = weights.astype(jnp.bfloat16)
        summed = jnp.zeros((rows, HD), jnp.float32)
        for b in range(n_blocks):
            summed = summed + jnp.dot(
                rounded[:, b * rows:(b + 1) * rows], kv_refs[b][1, :, cols], preferred_element_type=jnp.float32
            )
        if carry_in:
            totals = carried * total_in[:, g * HD:g * HD + 1] + totals
            summed = carried * acc_in[:, cols] + summed
        if finish:
            out_ref[:, cols] = (summed / totals).astype(out_ref.dtype)
        else:
            acc_out[:, cols] = summed
            peak_out[:, cols] = jnp.broadcast_to(peak, (rows, HD))
            total_out[:, cols] = jnp.broadcast_to(totals, (rows, HD))


def block_attention(queries, kv_list, flat_masks, carry=None, finish=True):
    rows, width = queries.shape
    heads = width // HD
    group = 5 if heads % 5 == 0 else 1
    n_blocks = len(kv_list)
    tiles = rows // TILE
    span = group * HD
    kv_spec = pl.BlockSpec((2, rows, span), lambda h, m: (0, 0, h))
    row_spec = pl.BlockSpec((rows, span), lambda h, m: (0, h))
    state_shape = jax.ShapeDtypeStruct((rows, width), jnp.float32)
    in_specs = [row_spec] + [kv_spec] * n_blocks
    operands = [flat_masks, queries, *kv_list]
    if carry is not None:
        in_specs += [row_spec] * 3
        operands += list(carry)
    if finish:
        out_shape = jax.ShapeDtypeStruct((rows, width), jnp.bfloat16)
        out_specs = row_spec
    else:
        out_shape = (state_shape,) * 3
        out_specs = (row_spec,) * 3
    grid_spec = pltpu.PrefetchScalarGridSpec(
        num_scalar_prefetch=1,
        grid=(heads // group,),
        in_specs=in_specs,
        out_specs=out_specs,
        scratch_shapes=[pltpu.VMEM((rows, n_blocks * rows), jnp.float32)],
    )
    flops = 4 * rows * n_blocks * rows * HD * heads
    bytes_moved = 2 * (rows * width * 2 + n_blocks * 2 * rows * width) + 24 * rows * width
    return pl.pallas_call(
        functools.partial(attention_kernel, n_blocks, tiles, group, carry is not None, finish),
        grid_spec=grid_spec,
        out_shape=out_shape,
        cost_estimate=pl.CostEstimate(
            flops=flops, transcendentals=rows * n_blocks * rows * heads, bytes_accessed=bytes_moved
        ),
    )(*operands)


def local(queries, keys, values, out_weight, tile_lists, tile_counts):
    tok_rows, feat_width = queries.shape
    tiles_here = tok_rows // TILE
    heads_here = feat_width // HD
    chips = lax.axis_size("chip")
    core = lax.axis_index("core")
    device_index = lax.axis_index("chip") * 2 + core
    query_heads = queries.reshape(tok_rows, heads_here, HD)
    stacked = jnp.stack([keys, values])
    own_lists = lax.dynamic_slice_in_dim(tile_lists, device_index * tiles_here, tiles_here, 0)
    own_counts = lax.dynamic_slice_in_dim(tile_counts, device_index * tiles_here, tiles_here, 0)
    live_slots = jnp.arange(own_lists.shape[1], dtype=jnp.int32)[None, :] < own_counts[:, None]

    def tile_need(offset):
        key_tiles = (device_index + offset) * tiles_here + jnp.arange(tiles_here, dtype=jnp.int32)
        matches = (own_lists[:, :, None] == key_tiles[None, None, :]) & live_slots[:, :, None]
        return jnp.any(matches, axis=1)

    early = [(0, stacked)]
    sibling = swapped(stacked, "core")
    early.append((1 - 2 * core, sibling))
    fetched = []
    for chip_step in (1, 2):
        for sign in (1, -1):
            block = shifted(stacked, "chip", sign * chip_step)
            fetched.append((-sign * 2 * chip_step, block))
            early.append((-sign * 2 * chip_step, block))
    from_below, from_above = fetched[0][1], fetched[1][1]
    onward = jnp.where(core == 1, from_below, from_above)
    two_below, two_above = fetched[2][1], fetched[3][1]
    across = jnp.where(core == 1, two_below, two_above)
    by_chip_hop, by_level_hop = fifth_routes(onward, across, chips)
    chip = lax.axis_index("chip")
    fifth = jnp.where((chip + core) % 2 == 0, by_chip_hop, by_level_hop)
    late = [(-REACH + 2 * REACH * core, fifth)]
    for offset, block in fetched:
        passed = swapped(block, "core")
        late.append((offset + 1 - 2 * core, passed))

    def masks_of(blocks):
        return jnp.stack([tile_need(offset) for offset, _ in blocks]).astype(jnp.int32).reshape(-1)

    carry = block_attention(queries, [b for _, b in early], masks_of(early), finish=False)
    attended = block_attention(queries, [b for _, b in late], masks_of(late), carry=carry)
    weight_rows = lax.all_gather(out_weight, SEQ, axis=1, tiled=True)
    heads = lax.axis_size("head")
    if heads == 2:
        half = weight_rows.shape[1] // 2
        me = lax.axis_index("head")
        mine = lax.dynamic_slice_in_dim(weight_rows, me * half, half, 1)
        theirs = lax.dynamic_slice_in_dim(weight_rows, (1 - me) * half, half, 1)
        parts = 4
        chunk = half // parts
        got = []
        for part in range(parts):
            cols = slice(part * chunk, (part + 1) * chunk)
            sent = jnp.dot(attended, theirs[:, cols], preferred_element_type=jnp.float32).astype(jnp.bfloat16)
            got.append(swapped(sent, "head"))
        kept_part = jnp.dot(attended, mine, preferred_element_type=jnp.float32).astype(jnp.bfloat16)
        kept_part = lax.optimization_barrier(kept_part)
        got = jnp.concatenate(got, axis=1)
        return (kept_part.astype(jnp.float32) + got.astype(jnp.float32)).astype(jnp.bfloat16)
    projected = jnp.dot(attended, weight_rows, preferred_element_type=jnp.float32)
    return lax.psum_scatter(projected.astype(jnp.bfloat16), "head", scatter_dimension=1, tiled=True)


def solution(mesh):
    heads = mesh.shape["head"]
    seq = mesh.shape["seq"]
    view = Mesh(mesh.devices.reshape(heads, seq // 2, 2), ("head", "chip", "core"))
    return jax.shard_map(
        local,
        mesh=view,
        in_specs=(P(SEQ, "head"), P(SEQ, "head"), P(SEQ, "head"), P("head", SEQ), P(), P()),
        out_specs=P(SEQ, "head"),
        check_vma=False,
    )
```

```python
import functools
import math

import jax
import jax.numpy as jnp
from jax import lax
from jax.experimental import pallas as pl
from jax.experimental.pallas import tpu as pltpu
from jax.sharding import Mesh
from jax.sharding import PartitionSpec as P

HD = 128
TILE = 128
REACH = 5

SEQ = ("chip", "core")

masked_floor = -1e30


def shifted(x, axis, by):
    peers = lax.axis_size(axis)
    pairs = [(i, i + by) for i in range(peers) if 0 <= i + by < peers]
    return lax.ppermute(x, axis, pairs)


def swapped(x, axis):
    return lax.ppermute(x, axis, [(0, 1), (1, 0)])


def third_neighbour(x, chips):
    peers = chips * 2
    pairs = []
    for s in range(peers):
        t = s + 3 if s % 2 == 1 else s - 3
        if 0 <= t < peers:
            pairs.append((s, t))
    return lax.ppermute(x, SEQ, pairs)


def attention_kernel(n_blocks, tiles, group, carry_in, finish, mask_ref, q_ref, *refs):
    kv_refs = refs[:n_blocks]
    at = n_blocks
    if carry_in:
        acc_in, peak_in, total_in = refs[at:at + 3]
        at += 3
    if finish:
        out_ref = refs[at]
        at += 1
    else:
        acc_out, peak_out, total_out = refs[at:at + 3]
        at += 3
    score_ref = refs[at]
    rows = q_ref.shape[0]
    for g in range(group):
        cols = slice(g * HD, (g + 1) * HD)
        query = q_ref[:, cols]
        for b in range(n_blocks):
            keys = kv_refs[b][0, :, cols]
            scores = lax.dot_general(
                query, keys, (((1,), (1,)), ((), ())), preferred_element_type=jnp.float32
            ) * (1.0 / math.sqrt(HD))
            for qi in range(tiles):
                for kt in range(tiles):
                    flag = mask_ref[(b * tiles + qi) * tiles + kt]
                    tile = scores[qi * TILE:(qi + 1) * TILE, kt * TILE:(kt + 1) * TILE]
                    score_ref[qi * TILE:(qi + 1) * TILE, b * rows + kt * TILE:b * rows + (kt + 1) * TILE] = (
                        jnp.where(flag != 0, tile, masked_floor)
                    )

        scores = score_ref[...]
        peak = jnp.max(scores, axis=1, keepdims=True)
        if carry_in:
            old_peak = peak_in[:, g * HD:g * HD + 1]
            peak = jnp.maximum(peak, old_peak)
            carried = jnp.exp(old_peak - peak)
        weights = jnp.exp(scores - peak)
        totals = jnp.sum(weights, axis=1, keepdims=True)
        rounded = weights.astype(jnp.bfloat16)
        summed = jnp.zeros((rows, HD), jnp.float32)
        for b in range(n_blocks):
            summed = summed + jnp.dot(
                rounded[:, b * rows:(b + 1) * rows], kv_refs[b][1, :, cols], preferred_element_type=jnp.float32
            )
        if carry_in:
            totals = carried * total_in[:, g * HD:g * HD + 1] + totals
            summed = carried * acc_in[:, cols] + summed
        if finish:
            out_ref[:, cols] = (summed / totals).astype(out_ref.dtype)
        else:
            acc_out[:, cols] = summed
            peak_out[:, cols] = jnp.broadcast_to(peak, (rows, HD))
            total_out[:, cols] = jnp.broadcast_to(totals, (rows, HD))


def block_attention(queries, kv_list, flat_masks, carry=None, finish=True):
    rows, width = queries.shape
    heads = width // HD
    group = 5 if heads % 5 == 0 else 1
    n_blocks = len(kv_list)
    tiles = rows // TILE
    span = group * HD
    kv_spec = pl.BlockSpec((2, rows, span), lambda h, m: (0, 0, h))
    row_spec = pl.BlockSpec((rows, span), lambda h, m: (0, h))
    state_shape = jax.ShapeDtypeStruct((rows, width), jnp.float32)
    in_specs = [row_spec] + [kv_spec] * n_blocks
    operands = [flat_masks, queries, *kv_list]
    if carry is not None:
        in_specs += [row_spec] * 3
        operands += list(carry)
    if finish:
        out_shape = jax.ShapeDtypeStruct((rows, width), jnp.bfloat16)
        out_specs = row_spec
    else:
        out_shape = (state_shape,) * 3
        out_specs = (row_spec,) * 3
    grid_spec = pltpu.PrefetchScalarGridSpec(
        num_scalar_prefetch=1,
        grid=(heads // group,),
        in_specs=in_specs,
        out_specs=out_specs,
        scratch_shapes=[pltpu.VMEM((rows, n_blocks * rows), jnp.float32)],
    )
    flops = 4 * rows * n_blocks * rows * HD * heads
    bytes_moved = 2 * (rows * width * 2 + n_blocks * 2 * rows * width) + 24 * rows * width
    return pl.pallas_call(
        functools.partial(attention_kernel, n_blocks, tiles, group, carry is not None, finish),
        grid_spec=grid_spec,
        out_shape=out_shape,
        cost_estimate=pl.CostEstimate(
            flops=flops, transcendentals=rows * n_blocks * rows * heads, bytes_accessed=bytes_moved
        ),
    )(*operands)


def local(queries, keys, values, out_weight, tile_lists, tile_counts):
    tok_rows, feat_width = queries.shape
    tiles_here = tok_rows // TILE
    heads_here = feat_width // HD
    chips = lax.axis_size("chip")
    core = lax.axis_index("core")
    device_index = lax.axis_index("chip") * 2 + core
    query_heads = queries.reshape(tok_rows, heads_here, HD)
    stacked = jnp.stack([keys, values])
    own_lists = lax.dynamic_slice_in_dim(tile_lists, device_index * tiles_here, tiles_here, 0)
    own_counts = lax.dynamic_slice_in_dim(tile_counts, device_index * tiles_here, tiles_here, 0)
    live_slots = jnp.arange(own_lists.shape[1], dtype=jnp.int32)[None, :] < own_counts[:, None]

    def tile_need(offset):
        key_tiles = (device_index + offset) * tiles_here + jnp.arange(tiles_here, dtype=jnp.int32)
        matches = (own_lists[:, :, None] == key_tiles[None, None, :]) & live_slots[:, :, None]
        return jnp.any(matches, axis=1)

    early = [(0, stacked)]
    sibling = swapped(stacked, "core")
    early.append((1 - 2 * core, sibling))
    fetched = []
    for chip_step in (1, 2):
        for sign in (1, -1):
            block = shifted(stacked, "chip", sign * chip_step)
            fetched.append((-sign * 2 * chip_step, block))
            early.append((-sign * 2 * chip_step, block))
    from_below, from_above = fetched[0][1], fetched[1][1]
    onward = jnp.where(core == 1, from_below, from_above)
    late = [(-REACH + 2 * REACH * core, third_neighbour(onward, chips))]
    for offset, block in fetched:
        passed = swapped(block, "core")
        early.append((offset + 1 - 2 * core, passed))

    def masks_of(blocks):
        return jnp.stack([tile_need(offset) for offset, _ in blocks]).astype(jnp.int32).reshape(-1)

    carry = block_attention(queries, [b for _, b in early], masks_of(early), finish=False)
    attended = block_attention(queries, [b for _, b in late], masks_of(late), carry=carry)
    weight_rows = lax.all_gather(out_weight, SEQ, axis=1, tiled=True)
    heads = lax.axis_size("head")
    if heads == 2:
        half = weight_rows.shape[1] // 2
        me = lax.axis_index("head")
        mine = lax.dynamic_slice_in_dim(weight_rows, me * half, half, 1)
        theirs = lax.dynamic_slice_in_dim(weight_rows, (1 - me) * half, half, 1)
        parts = 4
        chunk = half // parts
        got = []
        for part in range(parts):
            cols = slice(part * chunk, (part + 1) * chunk)
            sent = jnp.dot(attended, theirs[:, cols], preferred_element_type=jnp.float32).astype(jnp.bfloat16)
            got.append(swapped(sent, "head"))
        kept_part = jnp.dot(attended, mine, preferred_element_type=jnp.float32).astype(jnp.bfloat16)
        kept_part = lax.optimization_barrier(kept_part)
        got = jnp.concatenate(got, axis=1)
        return (kept_part.astype(jnp.float32) + got.astype(jnp.float32)).astype(jnp.bfloat16)
    projected = jnp.dot(attended, weight_rows, preferred_element_type=jnp.float32)
    return lax.psum_scatter(projected.astype(jnp.bfloat16), "head", scatter_dimension=1, tiled=True)


def solution(mesh):
    heads = mesh.shape["head"]
    seq = mesh.shape["seq"]
    view = Mesh(mesh.devices.reshape(heads, seq // 2, 2), ("head", "chip", "core"))
    return jax.shard_map(
        local,
        mesh=view,
        in_specs=(P(SEQ, "head"), P(SEQ, "head"), P(SEQ, "head"), P("head", SEQ), P(), P()),
        out_specs=P(SEQ, "head"),
        check_vma=False,
    )
```

```python
import functools
import math

import jax
import jax.numpy as jnp
from jax import lax
from jax.experimental import pallas as pl
from jax.experimental.pallas import tpu as pltpu
from jax.sharding import Mesh
from jax.sharding import PartitionSpec as P

HD = 128
TILE = 128
REACH = 5

SEQ = ("chip", "core")

masked_floor = -1e30


def shifted(x, axis, by):
    peers = lax.axis_size(axis)
    pairs = [(i, i + by) for i in range(peers) if 0 <= i + by < peers]
    return lax.ppermute(x, axis, pairs)


def swapped(x, axis):
    return lax.ppermute(x, axis, [(0, 1), (1, 0)])


def third_neighbours(from_below, from_above, chips):
    peers = chips * 2
    up = [(s, s + 3) for s in range(1, peers, 2) if s + 3 < peers]
    down = [(s, s - 3) for s in range(0, peers, 2) if s - 3 >= 0]
    return lax.ppermute(from_below, SEQ, up), lax.ppermute(from_above, SEQ, down)


def attention_kernel(n_blocks, tiles, group, carry_in, finish, mask_ref, q_ref, *refs):
    kv_refs = refs[:n_blocks]
    at = n_blocks
    if carry_in:
        acc_in, peak_in, total_in = refs[at:at + 3]
        at += 3
    if finish:
        out_ref = refs[at]
        at += 1
    else:
        acc_out, peak_out, total_out = refs[at:at + 3]
        at += 3
    score_ref = refs[at]
    rows = q_ref.shape[0]
    for g in range(group):
        cols = slice(g * HD, (g + 1) * HD)
        query = q_ref[:, cols]
        for b in range(n_blocks):
            keys = kv_refs[b][0, :, cols]
            scores = lax.dot_general(
                query, keys, (((1,), (1,)), ((), ())), preferred_element_type=jnp.float32
            ) * (1.0 / math.sqrt(HD))
            for qi in range(tiles):
                for kt in range(tiles):
                    flag = mask_ref[(b * tiles + qi) * tiles + kt]
                    tile = scores[qi * TILE:(qi + 1) * TILE, kt * TILE:(kt + 1) * TILE]
                    score_ref[qi * TILE:(qi + 1) * TILE, b * rows + kt * TILE:b * rows + (kt + 1) * TILE] = (
                        jnp.where(flag != 0, tile, masked_floor)
                    )

        scores = score_ref[...]
        peak = jnp.max(scores, axis=1, keepdims=True)
        if carry_in:
            old_peak = peak_in[:, g * HD:g * HD + 1]
            peak = jnp.maximum(peak, old_peak)
            carried = jnp.exp(old_peak - peak)
        weights = jnp.exp(scores - peak)
        totals = jnp.sum(weights, axis=1, keepdims=True)
        rounded = weights.astype(jnp.bfloat16)
        summed = jnp.zeros((rows, HD), jnp.float32)
        for b in range(n_blocks):
            summed = summed + jnp.dot(
                rounded[:, b * rows:(b + 1) * rows], kv_refs[b][1, :, cols], preferred_element_type=jnp.float32
            )
        if carry_in:
            totals = carried * total_in[:, g * HD:g * HD + 1] + totals
            summed = carried * acc_in[:, cols] + summed
        if finish:
            out_ref[:, cols] = (summed / totals).astype(out_ref.dtype)
        else:
            acc_out[:, cols] = summed
            peak_out[:, cols] = jnp.broadcast_to(peak, (rows, HD))
            total_out[:, cols] = jnp.broadcast_to(totals, (rows, HD))


def block_attention(queries, kv_list, flat_masks, carry=None, finish=True):
    rows, width = queries.shape
    heads = width // HD
    group = 5 if heads % 5 == 0 else 1
    n_blocks = len(kv_list)
    tiles = rows // TILE
    span = group * HD
    kv_spec = pl.BlockSpec((2, rows, span), lambda h, m: (0, 0, h))
    row_spec = pl.BlockSpec((rows, span), lambda h, m: (0, h))
    state_shape = jax.ShapeDtypeStruct((rows, width), jnp.float32)
    in_specs = [row_spec] + [kv_spec] * n_blocks
    operands = [flat_masks, queries, *kv_list]
    if carry is not None:
        in_specs += [row_spec] * 3
        operands += list(carry)
    if finish:
        out_shape = jax.ShapeDtypeStruct((rows, width), jnp.bfloat16)
        out_specs = row_spec
    else:
        out_shape = (state_shape,) * 3
        out_specs = (row_spec,) * 3
    grid_spec = pltpu.PrefetchScalarGridSpec(
        num_scalar_prefetch=1,
        grid=(heads // group,),
        in_specs=in_specs,
        out_specs=out_specs,
        scratch_shapes=[pltpu.VMEM((rows, n_blocks * rows), jnp.float32)],
    )
    flops = 4 * rows * n_blocks * rows * HD * heads
    bytes_moved = 2 * (rows * width * 2 + n_blocks * 2 * rows * width) + 24 * rows * width
    return pl.pallas_call(
        functools.partial(attention_kernel, n_blocks, tiles, group, carry is not None, finish),
        grid_spec=grid_spec,
        out_shape=out_shape,
        cost_estimate=pl.CostEstimate(
            flops=flops, transcendentals=rows * n_blocks * rows * heads, bytes_accessed=bytes_moved
        ),
    )(*operands)


def local(queries, keys, values, out_weight, tile_lists, tile_counts):
    tok_rows, feat_width = queries.shape
    tiles_here = tok_rows // TILE
    heads_here = feat_width // HD
    chips = lax.axis_size("chip")
    core = lax.axis_index("core")
    device_index = lax.axis_index("chip") * 2 + core
    query_heads = queries.reshape(tok_rows, heads_here, HD)
    stacked = jnp.stack([keys, values])
    own_lists = lax.dynamic_slice_in_dim(tile_lists, device_index * tiles_here, tiles_here, 0)
    own_counts = lax.dynamic_slice_in_dim(tile_counts, device_index * tiles_here, tiles_here, 0)
    live_slots = jnp.arange(own_lists.shape[1], dtype=jnp.int32)[None, :] < own_counts[:, None]

    def tile_need(offset):
        key_tiles = (device_index + offset) * tiles_here + jnp.arange(tiles_here, dtype=jnp.int32)
        matches = (own_lists[:, :, None] == key_tiles[None, None, :]) & live_slots[:, :, None]
        return jnp.any(matches, axis=1)

    early = [(0, stacked)]
    sibling = swapped(stacked, "core")
    early.append((1 - 2 * core, sibling))
    fetched = []
    for chip_step in (1, 2):
        for sign in (1, -1):
            block = shifted(stacked, "chip", sign * chip_step)
            fetched.append((-sign * 2 * chip_step, block))
            early.append((-sign * 2 * chip_step, block))
    from_below, from_above = fetched[0][1], fetched[1][1]
    up_three, down_three = third_neighbours(from_below, from_above, chips)
    late = [(-REACH, up_three, core == 0), (REACH, down_three, core == 1)]
    for offset, block in fetched:
        passed = swapped(block, "core")
        early.append((offset + 1 - 2 * core, passed))

    def masks_of(blocks):
        return jnp.stack([tile_need(offset) for offset, _ in blocks]).astype(jnp.int32).reshape(-1)

    late_masks = jnp.stack([tile_need(offset) & here for offset, _, here in late]).astype(jnp.int32).reshape(-1)
    carry = block_attention(queries, [b for _, b in early], masks_of(early), finish=False)
    attended = block_attention(queries, [b for _, b, _ in late], late_masks, carry=carry)
    weight_rows = lax.all_gather(out_weight, SEQ, axis=1, tiled=True)
    heads = lax.axis_size("head")
    if heads == 2:
        half = weight_rows.shape[1] // 2
        me = lax.axis_index("head")
        mine = lax.dynamic_slice_in_dim(weight_rows, me * half, half, 1)
        theirs = lax.dynamic_slice_in_dim(weight_rows, (1 - me) * half, half, 1)
        parts = 4
        chunk = half // parts
        got = []
        for part in range(parts):
            cols = slice(part * chunk, (part + 1) * chunk)
            sent = jnp.dot(attended, theirs[:, cols], preferred_element_type=jnp.float32).astype(jnp.bfloat16)
            got.append(swapped(sent, "head"))
        kept_part = jnp.dot(attended, mine, preferred_element_type=jnp.float32).astype(jnp.bfloat16)
        kept_part = lax.optimization_barrier(kept_part)
        got = jnp.concatenate(got, axis=1)
        return (kept_part.astype(jnp.float32) + got.astype(jnp.float32)).astype(jnp.bfloat16)
    projected = jnp.dot(attended, weight_rows, preferred_element_type=jnp.float32)
    return lax.psum_scatter(projected.astype(jnp.bfloat16), "head", scatter_dimension=1, tiled=True)


def solution(mesh):
    heads = mesh.shape["head"]
    seq = mesh.shape["seq"]
    view = Mesh(mesh.devices.reshape(heads, seq // 2, 2), ("head", "chip", "core"))
    return jax.shard_map(
        local,
        mesh=view,
        in_specs=(P(SEQ, "head"), P(SEQ, "head"), P(SEQ, "head"), P("head", SEQ), P(), P()),
        out_specs=P(SEQ, "head"),
        check_vma=False,
    )
```

```python
import functools
import math

import jax
import jax.numpy as jnp
from jax import lax
from jax.experimental import pallas as pl
from jax.experimental.pallas import tpu as pltpu
from jax.sharding import Mesh
from jax.sharding import PartitionSpec as P

HD = 128
TILE = 128
REACH = 5

SEQ = ("chip", "core")

masked_floor = -1e30


def shifted(x, axis, by):
    peers = lax.axis_size(axis)
    pairs = [(i, i + by) for i in range(peers) if 0 <= i + by < peers]
    return lax.ppermute(x, axis, pairs)


def swapped(x, axis):
    return lax.ppermute(x, axis, [(0, 1), (1, 0)])


def third_neighbours(from_below, from_above, chips):
    peers = chips * 2
    up = [(s, s + 3) for s in range(1, peers, 2) if s + 3 < peers]
    down = [(s, s - 3) for s in range(0, peers, 2) if s - 3 >= 0]
    return lax.ppermute(from_below, SEQ, up), lax.ppermute(from_above, SEQ, down)


def attention_kernel(n_blocks, tiles, group, carry_in, finish, mask_ref, q_ref, *refs):
    kv_refs = refs[:n_blocks]
    at = n_blocks
    if carry_in:
        acc_in, peak_in, total_in = refs[at:at + 3]
        at += 3
    if finish:
        out_ref = refs[at]
        at += 1
    else:
        acc_out, peak_out, total_out = refs[at:at + 3]
        at += 3
    score_ref = refs[at]
    rows = q_ref.shape[0]
    for g in range(group):
        cols = slice(g * HD, (g + 1) * HD)
        query = q_ref[:, cols]
        for b in range(n_blocks):
            keys = kv_refs[b][0, :, cols]
            scores = lax.dot_general(
                query, keys, (((1,), (1,)), ((), ())), preferred_element_type=jnp.float32
            )
            for qi in range(tiles):
                for kt in range(tiles):
                    flag = mask_ref[(b * tiles + qi) * tiles + kt]
                    tile = scores[qi * TILE:(qi + 1) * TILE, kt * TILE:(kt + 1) * TILE]
                    score_ref[qi * TILE:(qi + 1) * TILE, b * rows + kt * TILE:b * rows + (kt + 1) * TILE] = (
                        jnp.where(flag != 0, tile, masked_floor)
                    )

        scores = score_ref[...]
        peak = jnp.max(scores, axis=1, keepdims=True)
        if carry_in:
            old_peak = peak_in[:, g * HD:g * HD + 1]
            peak = jnp.maximum(peak, old_peak)
            carried = jnp.exp((old_peak - peak) * (1.0 / math.sqrt(HD)))
        scale = 1.0 / math.sqrt(HD)
        weights = jnp.exp(scores * scale - peak * scale)
        totals = jnp.sum(weights, axis=1, keepdims=True)
        rounded = weights.astype(jnp.bfloat16)
        summed = jnp.zeros((rows, HD), jnp.float32)
        for b in range(n_blocks):
            summed = summed + jnp.dot(
                rounded[:, b * rows:(b + 1) * rows], kv_refs[b][1, :, cols], preferred_element_type=jnp.float32
            )
        if carry_in:
            totals = carried * total_in[:, g * HD:g * HD + 1] + totals
            summed = carried * acc_in[:, cols] + summed
        if finish:
            out_ref[:, cols] = (summed / totals).astype(out_ref.dtype)
        else:
            acc_out[:, cols] = summed
            peak_out[:, cols] = jnp.broadcast_to(peak, (rows, HD))
            total_out[:, cols] = jnp.broadcast_to(totals, (rows, HD))


def block_attention(queries, kv_list, flat_masks, carry=None, finish=True):
    rows, width = queries.shape
    heads = width // HD
    group = 5 if heads % 5 == 0 else 1
    n_blocks = len(kv_list)
    tiles = rows // TILE
    span = group * HD
    kv_spec = pl.BlockSpec((2, rows, span), lambda h, m: (0, 0, h))
    row_spec = pl.BlockSpec((rows, span), lambda h, m: (0, h))
    state_shape = jax.ShapeDtypeStruct((rows, width), jnp.float32)
    in_specs = [row_spec] + [kv_spec] * n_blocks
    operands = [flat_masks, queries, *kv_list]
    if carry is not None:
        in_specs += [row_spec] * 3
        operands += list(carry)
    if finish:
        out_shape = jax.ShapeDtypeStruct((rows, width), jnp.bfloat16)
        out_specs = row_spec
    else:
        out_shape = (state_shape,) * 3
        out_specs = (row_spec,) * 3
    grid_spec = pltpu.PrefetchScalarGridSpec(
        num_scalar_prefetch=1,
        grid=(heads // group,),
        in_specs=in_specs,
        out_specs=out_specs,
        scratch_shapes=[pltpu.VMEM((rows, n_blocks * rows), jnp.float32)],
    )
    flops = 4 * rows * n_blocks * rows * HD * heads
    bytes_moved = 2 * (rows * width * 2 + n_blocks * 2 * rows * width) + 24 * rows * width
    return pl.pallas_call(
        functools.partial(attention_kernel, n_blocks, tiles, group, carry is not None, finish),
        grid_spec=grid_spec,
        out_shape=out_shape,
        cost_estimate=pl.CostEstimate(
            flops=flops, transcendentals=rows * n_blocks * rows * heads, bytes_accessed=bytes_moved
        ),
    )(*operands)


def local(queries, keys, values, out_weight, tile_lists, tile_counts):
    tok_rows, feat_width = queries.shape
    tiles_here = tok_rows // TILE
    heads_here = feat_width // HD
    chips = lax.axis_size("chip")
    core = lax.axis_index("core")
    device_index = lax.axis_index("chip") * 2 + core
    query_heads = queries.reshape(tok_rows, heads_here, HD)
    stacked = jnp.stack([keys, values])
    own_lists = lax.dynamic_slice_in_dim(tile_lists, device_index * tiles_here, tiles_here, 0)
    own_counts = lax.dynamic_slice_in_dim(tile_counts, device_index * tiles_here, tiles_here, 0)
    live_slots = jnp.arange(own_lists.shape[1], dtype=jnp.int32)[None, :] < own_counts[:, None]

    def tile_need(offset):
        key_tiles = (device_index + offset) * tiles_here + jnp.arange(tiles_here, dtype=jnp.int32)
        matches = (own_lists[:, :, None] == key_tiles[None, None, :]) & live_slots[:, :, None]
        return jnp.any(matches, axis=1)

    early = [(0, stacked)]
    sibling = swapped(stacked, "core")
    early.append((1 - 2 * core, sibling))
    fetched = []
    for chip_step in (1, 2):
        for sign in (1, -1):
            block = shifted(stacked, "chip", sign * chip_step)
            fetched.append((-sign * 2 * chip_step, block))
            early.append((-sign * 2 * chip_step, block))
    from_below, from_above = fetched[0][1], fetched[1][1]
    up_three, down_three = third_neighbours(from_below, from_above, chips)
    late = [(-REACH, up_three, core == 0), (REACH, down_three, core == 1)]
    for offset, block in fetched:
        passed = swapped(block, "core")
        early.append((offset + 1 - 2 * core, passed))

    def masks_of(blocks):
        return jnp.stack([tile_need(offset) for offset, _ in blocks]).astype(jnp.int32).reshape(-1)

    late_masks = jnp.stack([tile_need(offset) & here for offset, _, here in late]).astype(jnp.int32).reshape(-1)
    carry = block_attention(queries, [b for _, b in early], masks_of(early), finish=False)
    attended = block_attention(queries, [b for _, b, _ in late], late_masks, carry=carry)
    weight_rows = lax.all_gather(out_weight, SEQ, axis=1, tiled=True)
    heads = lax.axis_size("head")
    if heads == 2:
        half = weight_rows.shape[1] // 2
        me = lax.axis_index("head")
        mine = lax.dynamic_slice_in_dim(weight_rows, me * half, half, 1)
        theirs = lax.dynamic_slice_in_dim(weight_rows, (1 - me) * half, half, 1)
        parts = 4
        chunk = half // parts
        got = []
        for part in range(parts):
            cols = slice(part * chunk, (part + 1) * chunk)
            sent = jnp.dot(attended, theirs[:, cols], preferred_element_type=jnp.float32).astype(jnp.bfloat16)
            got.append(swapped(sent, "head"))
        kept_part = jnp.dot(attended, mine, preferred_element_type=jnp.float32).astype(jnp.bfloat16)
        kept_part = lax.optimization_barrier(kept_part)
        got = jnp.concatenate(got, axis=1)
        return (kept_part.astype(jnp.float32) + got.astype(jnp.float32)).astype(jnp.bfloat16)
    projected = jnp.dot(attended, weight_rows, preferred_element_type=jnp.float32)
    return lax.psum_scatter(projected.astype(jnp.bfloat16), "head", scatter_dimension=1, tiled=True)


def solution(mesh):
    heads = mesh.shape["head"]
    seq = mesh.shape["seq"]
    view = Mesh(mesh.devices.reshape(heads, seq // 2, 2), ("head", "chip", "core"))
    return jax.shard_map(
        local,
        mesh=view,
        in_specs=(P(SEQ, "head"), P(SEQ, "head"), P(SEQ, "head"), P("head", SEQ), P(), P()),
        out_specs=P(SEQ, "head"),
        check_vma=False,
    )
```

```python
import functools
import math

import jax
import jax.numpy as jnp
from jax import lax
from jax.experimental import pallas as pl
from jax.experimental.pallas import tpu as pltpu
from jax.sharding import Mesh
from jax.sharding import PartitionSpec as P

HD = 128
TILE = 128
REACH = 5

SEQ = ("chip", "core")

masked_floor = -1e30


def shifted(x, axis, by):
    peers = lax.axis_size(axis)
    pairs = [(i, i + by) for i in range(peers) if 0 <= i + by < peers]
    return lax.ppermute(x, axis, pairs)


def swapped(x, axis):
    return lax.ppermute(x, axis, [(0, 1), (1, 0)])


def third_neighbours(from_below, from_above, chips):
    peers = chips * 2
    up = [(s, s + 3) for s in range(1, peers, 2) if s + 3 < peers]
    down = [(s, s - 3) for s in range(0, peers, 2) if s - 3 >= 0]
    return lax.ppermute(from_below, SEQ, up), lax.ppermute(from_above, SEQ, down)


def attention_kernel(n_blocks, tiles, group, carry_in, finish, mask_ref, q_ref, *refs):
    kv_refs = refs[:n_blocks]
    at = n_blocks
    if carry_in:
        acc_in, stats_in = refs[at:at + 2]
        at += 2
    if finish:
        out_ref = refs[at]
        at += 1
    else:
        acc_out, stats_out = refs[at:at + 2]
        at += 2
    score_ref = refs[at]
    rows = q_ref.shape[0]
    for g in range(group):
        cols = slice(g * HD, (g + 1) * HD)
        query = q_ref[:, cols]
        for b in range(n_blocks):
            keys = kv_refs[b][0, :, cols]
            scores = lax.dot_general(
                query, keys, (((1,), (1,)), ((), ())), preferred_element_type=jnp.float32
            ) * (1.0 / math.sqrt(HD))
            for qi in range(tiles):
                for kt in range(tiles):
                    flag = mask_ref[(b * tiles + qi) * tiles + kt]
                    tile = scores[qi * TILE:(qi + 1) * TILE, kt * TILE:(kt + 1) * TILE]
                    score_ref[qi * TILE:(qi + 1) * TILE, b * rows + kt * TILE:b * rows + (kt + 1) * TILE] = (
                        jnp.where(flag != 0, tile, masked_floor)
                    )

        scores = score_ref[...]
        peak = jnp.max(scores, axis=1, keepdims=True)
        if carry_in:
            old_peak = stats_in[:, g * HD:g * HD + 1]
            peak = jnp.maximum(peak, old_peak)
            carried = jnp.exp(old_peak - peak)
        weights = jnp.exp(scores - peak)
        totals = jnp.sum(weights, axis=1, keepdims=True)
        rounded = weights.astype(jnp.bfloat16)
        summed = jnp.zeros((rows, HD), jnp.float32)
        for b in range(n_blocks):
            summed = summed + jnp.dot(
                rounded[:, b * rows:(b + 1) * rows], kv_refs[b][1, :, cols], preferred_element_type=jnp.float32
            )
        if carry_in:
            totals = carried * stats_in[:, g * HD + 1:g * HD + 2] + totals
            summed = carried * acc_in[:, cols] + summed
        if finish:
            out_ref[:, cols] = (summed / totals).astype(out_ref.dtype)
        else:
            acc_out[:, cols] = summed
            lane = lax.broadcasted_iota(jnp.int32, (rows, HD), 1)
            stats_out[:, cols] = jnp.where(
                lane == 0, jnp.broadcast_to(peak, (rows, HD)), jnp.broadcast_to(totals, (rows, HD))
            )


def block_attention(queries, kv_list, flat_masks, carry=None, finish=True):
    rows, width = queries.shape
    heads = width // HD
    group = 5 if heads % 5 == 0 else 1
    n_blocks = len(kv_list)
    tiles = rows // TILE
    span = group * HD
    kv_spec = pl.BlockSpec((2, rows, span), lambda h, m: (0, 0, h))
    row_spec = pl.BlockSpec((rows, span), lambda h, m: (0, h))
    state_shape = jax.ShapeDtypeStruct((rows, width), jnp.float32)
    in_specs = [row_spec] + [kv_spec] * n_blocks
    operands = [flat_masks, queries, *kv_list]
    if carry is not None:
        in_specs += [row_spec] * 2
        operands += list(carry)
    if finish:
        out_shape = jax.ShapeDtypeStruct((rows, width), jnp.bfloat16)
        out_specs = row_spec
    else:
        out_shape = (state_shape,) * 2
        out_specs = (row_spec,) * 2
    grid_spec = pltpu.PrefetchScalarGridSpec(
        num_scalar_prefetch=1,
        grid=(heads // group,),
        in_specs=in_specs,
        out_specs=out_specs,
        scratch_shapes=[pltpu.VMEM((rows, n_blocks * rows), jnp.float32)],
    )
    flops = 4 * rows * n_blocks * rows * HD * heads
    bytes_moved = 2 * (rows * width * 2 + n_blocks * 2 * rows * width) + 16 * rows * width
    return pl.pallas_call(
        functools.partial(attention_kernel, n_blocks, tiles, group, carry is not None, finish),
        grid_spec=grid_spec,
        out_shape=out_shape,
        cost_estimate=pl.CostEstimate(
            flops=flops, transcendentals=rows * n_blocks * rows * heads, bytes_accessed=bytes_moved
        ),
    )(*operands)


def local(queries, keys, values, out_weight, tile_lists, tile_counts):
    tok_rows, feat_width = queries.shape
    tiles_here = tok_rows // TILE
    heads_here = feat_width // HD
    chips = lax.axis_size("chip")
    core = lax.axis_index("core")
    device_index = lax.axis_index("chip") * 2 + core
    query_heads = queries.reshape(tok_rows, heads_here, HD)
    stacked = jnp.stack([keys, values])
    own_lists = lax.dynamic_slice_in_dim(tile_lists, device_index * tiles_here, tiles_here, 0)
    own_counts = lax.dynamic_slice_in_dim(tile_counts, device_index * tiles_here, tiles_here, 0)
    live_slots = jnp.arange(own_lists.shape[1], dtype=jnp.int32)[None, :] < own_counts[:, None]

    def tile_need(offset):
        key_tiles = (device_index + offset) * tiles_here + jnp.arange(tiles_here, dtype=jnp.int32)
        matches = (own_lists[:, :, None] == key_tiles[None, None, :]) & live_slots[:, :, None]
        return jnp.any(matches, axis=1)

    early = [(0, stacked)]
    sibling = swapped(stacked, "core")
    early.append((1 - 2 * core, sibling))
    fetched = []
    for chip_step in (1, 2):
        for sign in (1, -1):
            block = shifted(stacked, "chip", sign * chip_step)
            fetched.append((-sign * 2 * chip_step, block))
            early.append((-sign * 2 * chip_step, block))
    from_below, from_above = fetched[0][1], fetched[1][1]
    up_three, down_three = third_neighbours(from_below, from_above, chips)
    late = [(-REACH, up_three, core == 0), (REACH, down_three, core == 1)]
    for offset, block in fetched:
        passed = swapped(block, "core")
        early.append((offset + 1 - 2 * core, passed))

    def masks_of(blocks):
        return jnp.stack([tile_need(offset) for offset, _ in blocks]).astype(jnp.int32).reshape(-1)

    late_masks = jnp.stack([tile_need(offset) & here for offset, _, here in late]).astype(jnp.int32).reshape(-1)
    carry = block_attention(queries, [b for _, b in early], masks_of(early), finish=False)
    attended = block_attention(queries, [b for _, b, _ in late], late_masks, carry=carry)
    weight_rows = lax.all_gather(out_weight, SEQ, axis=1, tiled=True)
    heads = lax.axis_size("head")
    if heads == 2:
        half = weight_rows.shape[1] // 2
        me = lax.axis_index("head")
        mine = lax.dynamic_slice_in_dim(weight_rows, me * half, half, 1)
        theirs = lax.dynamic_slice_in_dim(weight_rows, (1 - me) * half, half, 1)
        parts = 4
        chunk = half // parts
        got = []
        for part in range(parts):
            cols = slice(part * chunk, (part + 1) * chunk)
            sent = jnp.dot(attended, theirs[:, cols], preferred_element_type=jnp.float32).astype(jnp.bfloat16)
            got.append(swapped(sent, "head"))
        kept_part = jnp.dot(attended, mine, preferred_element_type=jnp.float32).astype(jnp.bfloat16)
        kept_part = lax.optimization_barrier(kept_part)
        got = jnp.concatenate(got, axis=1)
        return (kept_part.astype(jnp.float32) + got.astype(jnp.float32)).astype(jnp.bfloat16)
    projected = jnp.dot(attended, weight_rows, preferred_element_type=jnp.float32)
    return lax.psum_scatter(projected.astype(jnp.bfloat16), "head", scatter_dimension=1, tiled=True)


def solution(mesh):
    heads = mesh.shape["head"]
    seq = mesh.shape["seq"]
    view = Mesh(mesh.devices.reshape(heads, seq // 2, 2), ("head", "chip", "core"))
    return jax.shard_map(
        local,
        mesh=view,
        in_specs=(P(SEQ, "head"), P(SEQ, "head"), P(SEQ, "head"), P("head", SEQ), P(), P()),
        out_specs=P(SEQ, "head"),
        check_vma=False,
    )
```

```python
import functools
import math

import jax
import jax.numpy as jnp
from jax import lax
from jax.experimental import pallas as pl
from jax.experimental.pallas import tpu as pltpu
from jax.sharding import Mesh
from jax.sharding import PartitionSpec as P

HD = 128
TILE = 128
REACH = 5

SEQ = ("chip", "core")

masked_floor = -1e30


def shifted(x, axis, by):
    peers = lax.axis_size(axis)
    pairs = [(i, i + by) for i in range(peers) if 0 <= i + by < peers]
    return lax.ppermute(x, axis, pairs)


def swapped(x, axis):
    return lax.ppermute(x, axis, [(0, 1), (1, 0)])


def third_neighbours(from_below, from_above, chips):
    peers = chips * 2
    up = [(s, s + 3) for s in range(1, peers, 2) if s + 3 < peers]
    down = [(s, s - 3) for s in range(0, peers, 2) if s - 3 >= 0]
    return lax.ppermute(from_below, SEQ, up), lax.ppermute(from_above, SEQ, down)


def attention_kernel(n_blocks, tiles, group, carry_in, finish, mask_ref, q_ref, *refs):
    kv_refs = refs[:n_blocks]
    at = n_blocks
    if carry_in:
        acc_in, stats_in = refs[at:at + 2]
        at += 2
    if finish:
        out_ref = refs[at]
        at += 1
    else:
        acc_out, stats_out = refs[at:at + 2]
        at += 2
    score_ref = refs[at]
    rows = q_ref.shape[0]
    for g in range(group):
        cols = slice(g * HD, (g + 1) * HD)
        query = q_ref[:, cols]
        for b in range(n_blocks):
            keys = kv_refs[b][0, :, cols]
            scores = lax.dot_general(
                query, keys, (((1,), (1,)), ((), ())), preferred_element_type=jnp.float32
            ) * (1.0 / math.sqrt(HD))
            for qi in range(tiles):
                for kt in range(tiles):
                    flag = mask_ref[(b * tiles + qi) * tiles + kt]
                    tile = scores[qi * TILE:(qi + 1) * TILE, kt * TILE:(kt + 1) * TILE]
                    score_ref[qi * TILE:(qi + 1) * TILE, b * rows + kt * TILE:b * rows + (kt + 1) * TILE] = (
                        jnp.where(flag != 0, tile, masked_floor)
                    )

        scores = score_ref[...]
        peak = jnp.max(scores, axis=1, keepdims=True)
        if carry_in:
            old_peak = stats_in[:, g * HD:g * HD + 1]
            peak = jnp.maximum(peak, old_peak)
            carried = jnp.exp(old_peak - peak)
        weights = jnp.exp(scores - peak)
        totals = jnp.sum(weights, axis=1, keepdims=True)
        rounded = weights.astype(jnp.bfloat16)
        summed = jnp.zeros((rows, HD), jnp.float32)
        for b in range(n_blocks):
            summed = summed + jnp.dot(
                rounded[:, b * rows:(b + 1) * rows], kv_refs[b][1, :, cols], preferred_element_type=jnp.float32
            )
        if carry_in:
            totals = carried * stats_in[:, g * HD + 1:g * HD + 2] + totals
            summed = carried * acc_in[:, cols] + summed
        if finish:
            out_ref[:, cols] = (summed / totals).astype(out_ref.dtype)
        else:
            acc_out[:, cols] = summed
            lane = lax.broadcasted_iota(jnp.int32, (rows, HD), 1)
            stats_out[:, cols] = jnp.where(
                lane == 0, jnp.broadcast_to(peak, (rows, HD)), jnp.broadcast_to(totals, (rows, HD))
            )


def block_attention(queries, kv_list, flat_masks, carry=None, finish=True):
    rows, width = queries.shape
    heads = width // HD
    group = 5 if heads % 5 == 0 else 1
    n_blocks = len(kv_list)
    tiles = rows // TILE
    span = group * HD
    kv_spec = pl.BlockSpec((2, rows, span), lambda h, m: (0, 0, h))
    row_spec = pl.BlockSpec((rows, span), lambda h, m: (0, h))
    state_shape = jax.ShapeDtypeStruct((rows, width), jnp.float32)
    in_specs = [row_spec] + [kv_spec] * n_blocks
    operands = [flat_masks, queries, *kv_list]
    if carry is not None:
        in_specs += [row_spec] * 2
        operands += list(carry)
    if finish:
        out_shape = jax.ShapeDtypeStruct((rows, width), jnp.bfloat16)
        out_specs = row_spec
    else:
        out_shape = (state_shape,) * 2
        out_specs = (row_spec,) * 2
    grid_spec = pltpu.PrefetchScalarGridSpec(
        num_scalar_prefetch=1,
        grid=(heads // group,),
        in_specs=in_specs,
        out_specs=out_specs,
        scratch_shapes=[pltpu.VMEM((rows, n_blocks * rows), jnp.float32)],
    )
    flops = 4 * rows * n_blocks * rows * HD * heads
    bytes_moved = 2 * (rows * width * 2 + n_blocks * 2 * rows * width) + 16 * rows * width
    return pl.pallas_call(
        functools.partial(attention_kernel, n_blocks, tiles, group, carry is not None, finish),
        grid_spec=grid_spec,
        out_shape=out_shape,
        cost_estimate=pl.CostEstimate(
            flops=flops, transcendentals=rows * n_blocks * rows * heads, bytes_accessed=bytes_moved
        ),
    )(*operands)


def local(queries, keys, values, out_weight, tile_lists, tile_counts):
    tok_rows, feat_width = queries.shape
    tiles_here = tok_rows // TILE
    heads_here = feat_width // HD
    chips = lax.axis_size("chip")
    core = lax.axis_index("core")
    device_index = lax.axis_index("chip") * 2 + core
    query_heads = queries.reshape(tok_rows, heads_here, HD)
    stacked = jnp.stack([keys, values])
    own_lists = lax.dynamic_slice_in_dim(tile_lists, device_index * tiles_here, tiles_here, 0)
    own_counts = lax.dynamic_slice_in_dim(tile_counts, device_index * tiles_here, tiles_here, 0)
    live_slots = jnp.arange(own_lists.shape[1], dtype=jnp.int32)[None, :] < own_counts[:, None]

    def tile_need(offset):
        key_tiles = (device_index + offset) * tiles_here + jnp.arange(tiles_here, dtype=jnp.int32)
        matches = (own_lists[:, :, None] == key_tiles[None, None, :]) & live_slots[:, :, None]
        return jnp.any(matches, axis=1)

    early = [(0, stacked)]
    sibling = swapped(stacked, "core")
    early.append((1 - 2 * core, sibling))
    fetched = []
    for chip_step in (1, 2):
        for sign in (1, -1):
            block = shifted(stacked, "chip", sign * chip_step)
            fetched.append((-sign * 2 * chip_step, block))
            early.append((-sign * 2 * chip_step, block))
    from_below, from_above = fetched[0][1], fetched[1][1]
    up_three, down_three = third_neighbours(from_below, from_above, chips)
    late = [(-REACH + 2 * REACH * core, up_three + down_three, True)]
    for offset, block in fetched:
        passed = swapped(block, "core")
        early.append((offset + 1 - 2 * core, passed))

    def masks_of(blocks):
        return jnp.stack([tile_need(offset) for offset, _ in blocks]).astype(jnp.int32).reshape(-1)

    late_masks = jnp.stack([tile_need(offset) & here for offset, _, here in late]).astype(jnp.int32).reshape(-1)
    carry = block_attention(queries, [b for _, b in early], masks_of(early), finish=False)
    attended = block_attention(queries, [b for _, b, _ in late], late_masks, carry=carry)
    weight_rows = lax.all_gather(out_weight, SEQ, axis=1, tiled=True)
    heads = lax.axis_size("head")
    if heads == 2:
        half = weight_rows.shape[1] // 2
        me = lax.axis_index("head")
        mine = lax.dynamic_slice_in_dim(weight_rows, me * half, half, 1)
        theirs = lax.dynamic_slice_in_dim(weight_rows, (1 - me) * half, half, 1)
        parts = 4
        chunk = half // parts
        got = []
        for part in range(parts):
            cols = slice(part * chunk, (part + 1) * chunk)
            sent = jnp.dot(attended, theirs[:, cols], preferred_element_type=jnp.float32).astype(jnp.bfloat16)
            got.append(swapped(sent, "head"))
        kept_part = jnp.dot(attended, mine, preferred_element_type=jnp.float32).astype(jnp.bfloat16)
        kept_part = lax.optimization_barrier(kept_part)
        got = jnp.concatenate(got, axis=1)
        return (kept_part.astype(jnp.float32) + got.astype(jnp.float32)).astype(jnp.bfloat16)
    projected = jnp.dot(attended, weight_rows, preferred_element_type=jnp.float32)
    return lax.psum_scatter(projected.astype(jnp.bfloat16), "head", scatter_dimension=1, tiled=True)


def solution(mesh):
    heads = mesh.shape["head"]
    seq = mesh.shape["seq"]
    view = Mesh(mesh.devices.reshape(heads, seq // 2, 2), ("head", "chip", "core"))
    return jax.shard_map(
        local,
        mesh=view,
        in_specs=(P(SEQ, "head"), P(SEQ, "head"), P(SEQ, "head"), P("head", SEQ), P(), P()),
        out_specs=P(SEQ, "head"),
        check_vma=False,
    )
```

```python
import functools
import math

import jax
import jax.numpy as jnp
from jax import lax
from jax.experimental import pallas as pl
from jax.experimental.pallas import tpu as pltpu
from jax.sharding import Mesh
from jax.sharding import PartitionSpec as P

HD = 128
TILE = 128
REACH = 5

SEQ = ("chip", "core")

masked_floor = -1e30


def shifted(x, axis, by):
    peers = lax.axis_size(axis)
    pairs = [(i, i + by) for i in range(peers) if 0 <= i + by < peers]
    return lax.ppermute(x, axis, pairs)


def swapped(x, axis):
    return lax.ppermute(x, axis, [(0, 1), (1, 0)])


def third_neighbours(from_below, from_above, chips):
    peers = chips * 2
    up = [(s, s + 3) for s in range(1, peers, 2) if s + 3 < peers]
    down = [(s, s - 3) for s in range(0, peers, 2) if s - 3 >= 0]
    return lax.ppermute(from_below, SEQ, up), lax.ppermute(from_above, SEQ, down)


def attention_kernel(n_blocks, tiles, group, carry_in, finish, mask_ref, q_ref, *refs):
    kv_refs = refs[:n_blocks]
    at = n_blocks
    if carry_in:
        acc_in, stats_in = refs[at:at + 2]
        at += 2
    if finish:
        out_ref = refs[at]
        at += 1
    else:
        acc_out, stats_out = refs[at:at + 2]
        at += 2
    score_ref = refs[at]
    rows = q_ref.shape[0]
    for g in range(group):
        cols = slice(g * HD, (g + 1) * HD)
        query = q_ref[:, cols]
        for b in range(n_blocks):
            keys = kv_refs[b][0, :, cols]
            scores = lax.dot_general(
                query, keys, (((1,), (1,)), ((), ())), preferred_element_type=jnp.float32
            ) * (1.0 / math.sqrt(HD))
            for qi in range(tiles):
                for kt in range(tiles):
                    flag = mask_ref[(b * tiles + qi) * tiles + kt]
                    tile = scores[qi * TILE:(qi + 1) * TILE, kt * TILE:(kt + 1) * TILE]
                    score_ref[qi * TILE:(qi + 1) * TILE, b * rows + kt * TILE:b * rows + (kt + 1) * TILE] = (
                        jnp.where(flag != 0, tile, masked_floor)
                    )

        scores = score_ref[...]
        peak = jnp.max(scores, axis=1, keepdims=True)
        if carry_in:
            old_peak = stats_in[:, g * HD:g * HD + 1]
            peak = jnp.maximum(peak, old_peak)
            carried = jnp.exp(old_peak - peak)
        weights = jnp.exp(scores - peak)
        totals = jnp.sum(weights, axis=1, keepdims=True)
        rounded = weights.astype(jnp.bfloat16)
        summed = jnp.zeros((rows, HD), jnp.float32)
        for b in range(n_blocks):
            summed = summed + jnp.dot(
                rounded[:, b * rows:(b + 1) * rows], kv_refs[b][1, :, cols], preferred_element_type=jnp.float32
            )
        if carry_in:
            totals = carried * stats_in[:, g * HD + 1:g * HD + 2] + totals
            summed = carried * acc_in[:, cols] + summed
        if finish:
            out_ref[:, cols] = (summed / totals).astype(out_ref.dtype)
        else:
            acc_out[:, cols] = summed
            lane = lax.broadcasted_iota(jnp.int32, (rows, HD), 1)
            stats_out[:, cols] = jnp.where(
                lane == 0, jnp.broadcast_to(peak, (rows, HD)), jnp.broadcast_to(totals, (rows, HD))
            )


def block_attention(queries, kv_list, flat_masks, carry=None, finish=True):
    rows, width = queries.shape
    heads = width // HD
    group = 5 if heads % 5 == 0 else 1
    n_blocks = len(kv_list)
    tiles = rows // TILE
    span = group * HD
    kv_spec = pl.BlockSpec((2, rows, span), lambda h, m: (0, 0, h))
    row_spec = pl.BlockSpec((rows, span), lambda h, m: (0, h))
    state_shape = jax.ShapeDtypeStruct((rows, width), jnp.float32)
    in_specs = [row_spec] + [kv_spec] * n_blocks
    operands = [flat_masks, queries, *kv_list]
    if carry is not None:
        in_specs += [row_spec] * 2
        operands += list(carry)
    if finish:
        out_shape = jax.ShapeDtypeStruct((rows, width), jnp.bfloat16)
        out_specs = row_spec
    else:
        out_shape = (state_shape,) * 2
        out_specs = (row_spec,) * 2
    grid_spec = pltpu.PrefetchScalarGridSpec(
        num_scalar_prefetch=1,
        grid=(heads // group,),
        in_specs=in_specs,
        out_specs=out_specs,
        scratch_shapes=[pltpu.VMEM((rows, n_blocks * rows), jnp.float32)],
    )
    flops = 4 * rows * n_blocks * rows * HD * heads
    bytes_moved = 2 * (rows * width * 2 + n_blocks * 2 * rows * width) + 16 * rows * width
    return pl.pallas_call(
        functools.partial(attention_kernel, n_blocks, tiles, group, carry is not None, finish),
        grid_spec=grid_spec,
        out_shape=out_shape,
        cost_estimate=pl.CostEstimate(
            flops=flops, transcendentals=rows * n_blocks * rows * heads, bytes_accessed=bytes_moved
        ),
    )(*operands)


def local(queries, keys, values, out_weight, tile_lists, tile_counts):
    tok_rows, feat_width = queries.shape
    tiles_here = tok_rows // TILE
    heads_here = feat_width // HD
    chips = lax.axis_size("chip")
    core = lax.axis_index("core")
    device_index = lax.axis_index("chip") * 2 + core
    query_heads = queries.reshape(tok_rows, heads_here, HD)
    stacked = jnp.stack([keys, values])
    own_lists = lax.dynamic_slice_in_dim(tile_lists, device_index * tiles_here, tiles_here, 0)
    own_counts = lax.dynamic_slice_in_dim(tile_counts, device_index * tiles_here, tiles_here, 0)
    live_slots = jnp.arange(own_lists.shape[1], dtype=jnp.int32)[None, :] < own_counts[:, None]

    def tile_need(offset):
        key_tiles = (device_index + offset) * tiles_here + jnp.arange(tiles_here, dtype=jnp.int32)
        matches = (own_lists[:, :, None] == key_tiles[None, None, :]) & live_slots[:, :, None]
        return jnp.any(matches, axis=1)

    early = [(0, stacked)]
    sibling = swapped(stacked, "core")
    early.append((1 - 2 * core, sibling))
    fetched = []
    for chip_step in (1, 2):
        for sign in (1, -1):
            block = shifted(stacked, "chip", sign * chip_step)
            fetched.append((-sign * 2 * chip_step, block))
            early.append((-sign * 2 * chip_step, block))
    from_below, from_above = fetched[0][1], fetched[1][1]
    up_three, down_three = third_neighbours(from_below, from_above, chips)
    late = [(-REACH, up_three, core == 0), (REACH, down_three, core == 1)]
    for offset, block in fetched:
        passed = swapped(block, "core")
        early.append((offset + 1 - 2 * core, passed))

    def masks_of(blocks):
        return jnp.stack([tile_need(offset) for offset, _ in blocks]).astype(jnp.int32).reshape(-1)

    late_masks = jnp.stack([tile_need(offset) & here for offset, _, here in late]).astype(jnp.int32).reshape(-1)
    carry = block_attention(queries, [b for _, b in early], masks_of(early), finish=False)
    attended = block_attention(queries, [b for _, b, _ in late], late_masks, carry=carry)
    weight_rows = lax.all_gather(out_weight, SEQ, axis=1, tiled=True)
    heads = lax.axis_size("head")
    if heads == 2:
        half = weight_rows.shape[1] // 2
        me = lax.axis_index("head")
        mine = lax.dynamic_slice_in_dim(weight_rows, me * half, half, 1)
        theirs = lax.dynamic_slice_in_dim(weight_rows, (1 - me) * half, half, 1)
        parts = 8
        chunk = half // parts
        got = []
        for part in range(parts):
            cols = slice(part * chunk, (part + 1) * chunk)
            sent = jnp.dot(attended, theirs[:, cols], preferred_element_type=jnp.float32).astype(jnp.bfloat16)
            got.append(swapped(sent, "head"))
        kept_part = jnp.dot(attended, mine, preferred_element_type=jnp.float32).astype(jnp.bfloat16)
        kept_part = lax.optimization_barrier(kept_part)
        got = jnp.concatenate(got, axis=1)
        return (kept_part.astype(jnp.float32) + got.astype(jnp.float32)).astype(jnp.bfloat16)
    projected = jnp.dot(attended, weight_rows, preferred_element_type=jnp.float32)
    return lax.psum_scatter(projected.astype(jnp.bfloat16), "head", scatter_dimension=1, tiled=True)


def solution(mesh):
    heads = mesh.shape["head"]
    seq = mesh.shape["seq"]
    view = Mesh(mesh.devices.reshape(heads, seq // 2, 2), ("head", "chip", "core"))
    return jax.shard_map(
        local,
        mesh=view,
        in_specs=(P(SEQ, "head"), P(SEQ, "head"), P(SEQ, "head"), P("head", SEQ), P(), P()),
        out_specs=P(SEQ, "head"),
        check_vma=False,
    )
```

```python
import functools
import math

import jax
import jax.numpy as jnp
from jax import lax
from jax.experimental import pallas as pl
from jax.experimental.pallas import tpu as pltpu
from jax.sharding import Mesh
from jax.sharding import PartitionSpec as P

HD = 128
TILE = 128
REACH = 5

SEQ = ("chip", "core")

masked_floor = -1e30


def shifted(x, axis, by):
    peers = lax.axis_size(axis)
    pairs = [(i, i + by) for i in range(peers) if 0 <= i + by < peers]
    return lax.ppermute(x, axis, pairs)


def swapped(x, axis):
    return lax.ppermute(x, axis, [(0, 1), (1, 0)])


def third_neighbours(from_below, from_above, chips):
    peers = chips * 2
    up = [(s, s + 3) for s in range(1, peers, 2) if s + 3 < peers]
    down = [(s, s - 3) for s in range(0, peers, 2) if s - 3 >= 0]
    return lax.ppermute(from_below, SEQ, up), lax.ppermute(from_above, SEQ, down)


def attention_kernel(n_blocks, tiles, group, carry_in, finish, mask_ref, q_ref, *refs):
    kv_refs = refs[:n_blocks]
    at = n_blocks
    if carry_in:
        acc_in, stats_in = refs[at:at + 2]
        at += 2
    if finish:
        out_ref = refs[at]
        at += 1
    else:
        acc_out, stats_out = refs[at:at + 2]
        at += 2
    score_ref = refs[at]
    rows = q_ref.shape[0]
    for g in range(group):
        cols = slice(g * HD, (g + 1) * HD)
        query = q_ref[:, cols]
        for b in range(n_blocks):
            keys = kv_refs[b][0, :, cols]
            scores = lax.dot_general(
                query, keys, (((1,), (1,)), ((), ())), preferred_element_type=jnp.float32
            ) * (1.0 / math.sqrt(HD))
            for qi in range(tiles):
                for kt in range(tiles):
                    flag = mask_ref[(b * tiles + qi) * tiles + kt]
                    tile = scores[qi * TILE:(qi + 1) * TILE, kt * TILE:(kt + 1) * TILE]
                    score_ref[qi * TILE:(qi + 1) * TILE, b * rows + kt * TILE:b * rows + (kt + 1) * TILE] = (
                        jnp.where(flag != 0, tile, masked_floor)
                    )

        scores = score_ref[...]
        peak = jnp.max(scores, axis=1, keepdims=True)
        if carry_in:
            old_peak = stats_in[:, g * HD:g * HD + 1]
            peak = jnp.maximum(peak, old_peak)
            carried = jnp.exp(old_peak - peak)
        weights = jnp.exp(scores - peak)
        totals = jnp.sum(weights, axis=1, keepdims=True)
        rounded = weights.astype(jnp.bfloat16)
        summed = jnp.zeros((rows, HD), jnp.float32)
        for b in range(n_blocks):
            summed = summed + jnp.dot(
                rounded[:, b * rows:(b + 1) * rows], kv_refs[b][1, :, cols], preferred_element_type=jnp.float32
            )
        if carry_in:
            totals = carried * stats_in[:, g * HD + 1:g * HD + 2] + totals
            summed = carried * acc_in[:, cols] + summed
        if finish:
            out_ref[:, cols] = (summed / totals).astype(out_ref.dtype)
        else:
            acc_out[:, cols] = summed
            lane = lax.broadcasted_iota(jnp.int32, (rows, HD), 1)
            stats_out[:, cols] = jnp.where(
                lane == 0, jnp.broadcast_to(peak, (rows, HD)), jnp.broadcast_to(totals, (rows, HD))
            )


def block_attention(queries, kv_list, flat_masks, carry=None, finish=True, per_step=5):
    rows, width = queries.shape
    heads = width // HD
    group = per_step if heads % per_step == 0 else (5 if heads % 5 == 0 else 1)
    n_blocks = len(kv_list)
    tiles = rows // TILE
    span = group * HD
    kv_spec = pl.BlockSpec((2, rows, span), lambda h, m: (0, 0, h))
    row_spec = pl.BlockSpec((rows, span), lambda h, m: (0, h))
    state_shape = jax.ShapeDtypeStruct((rows, width), jnp.float32)
    in_specs = [row_spec] + [kv_spec] * n_blocks
    operands = [flat_masks, queries, *kv_list]
    if carry is not None:
        in_specs += [row_spec] * 2
        operands += list(carry)
    if finish:
        out_shape = jax.ShapeDtypeStruct((rows, width), jnp.bfloat16)
        out_specs = row_spec
    else:
        out_shape = (state_shape,) * 2
        out_specs = (row_spec,) * 2
    grid_spec = pltpu.PrefetchScalarGridSpec(
        num_scalar_prefetch=1,
        grid=(heads // group,),
        in_specs=in_specs,
        out_specs=out_specs,
        scratch_shapes=[pltpu.VMEM((rows, n_blocks * rows), jnp.float32)],
    )
    flops = 4 * rows * n_blocks * rows * HD * heads
    bytes_moved = 2 * (rows * width * 2 + n_blocks * 2 * rows * width) + 16 * rows * width
    return pl.pallas_call(
        functools.partial(attention_kernel, n_blocks, tiles, group, carry is not None, finish),
        grid_spec=grid_spec,
        out_shape=out_shape,
        cost_estimate=pl.CostEstimate(
            flops=flops, transcendentals=rows * n_blocks * rows * heads, bytes_accessed=bytes_moved
        ),
    )(*operands)


def local(queries, keys, values, out_weight, tile_lists, tile_counts):
    tok_rows, feat_width = queries.shape
    tiles_here = tok_rows // TILE
    heads_here = feat_width // HD
    chips = lax.axis_size("chip")
    core = lax.axis_index("core")
    device_index = lax.axis_index("chip") * 2 + core
    query_heads = queries.reshape(tok_rows, heads_here, HD)
    stacked = jnp.stack([keys, values])
    own_lists = lax.dynamic_slice_in_dim(tile_lists, device_index * tiles_here, tiles_here, 0)
    own_counts = lax.dynamic_slice_in_dim(tile_counts, device_index * tiles_here, tiles_here, 0)
    live_slots = jnp.arange(own_lists.shape[1], dtype=jnp.int32)[None, :] < own_counts[:, None]

    def tile_need(offset):
        key_tiles = (device_index + offset) * tiles_here + jnp.arange(tiles_here, dtype=jnp.int32)
        matches = (own_lists[:, :, None] == key_tiles[None, None, :]) & live_slots[:, :, None]
        return jnp.any(matches, axis=1)

    early = [(0, stacked)]
    sibling = swapped(stacked, "core")
    early.append((1 - 2 * core, sibling))
    fetched = []
    for chip_step in (1, 2):
        for sign in (1, -1):
            block = shifted(stacked, "chip", sign * chip_step)
            fetched.append((-sign * 2 * chip_step, block))
            early.append((-sign * 2 * chip_step, block))
    from_below, from_above = fetched[0][1], fetched[1][1]
    up_three, down_three = third_neighbours(from_below, from_above, chips)
    late = [(-REACH, up_three, core == 0), (REACH, down_three, core == 1)]
    for offset, block in fetched:
        passed = swapped(block, "core")
        early.append((offset + 1 - 2 * core, passed))

    def masks_of(blocks):
        return jnp.stack([tile_need(offset) for offset, _ in blocks]).astype(jnp.int32).reshape(-1)

    late_masks = jnp.stack([tile_need(offset) & here for offset, _, here in late]).astype(jnp.int32).reshape(-1)
    carry = block_attention(queries, [b for _, b in early], masks_of(early), finish=False)
    attended = block_attention(queries, [b for _, b, _ in late], late_masks, carry=carry, per_step=10)
    weight_rows = lax.all_gather(out_weight, SEQ, axis=1, tiled=True)
    heads = lax.axis_size("head")
    if heads == 2:
        half = weight_rows.shape[1] // 2
        me = lax.axis_index("head")
        mine = lax.dynamic_slice_in_dim(weight_rows, me * half, half, 1)
        theirs = lax.dynamic_slice_in_dim(weight_rows, (1 - me) * half, half, 1)
        parts = 4
        chunk = half // parts
        got = []
        for part in range(parts):
            cols = slice(part * chunk, (part + 1) * chunk)
            sent = jnp.dot(attended, theirs[:, cols], preferred_element_type=jnp.float32).astype(jnp.bfloat16)
            got.append(swapped(sent, "head"))
        kept_part = jnp.dot(attended, mine, preferred_element_type=jnp.float32).astype(jnp.bfloat16)
        kept_part = lax.optimization_barrier(kept_part)
        got = jnp.concatenate(got, axis=1)
        return (kept_part.astype(jnp.float32) + got.astype(jnp.float32)).astype(jnp.bfloat16)
    projected = jnp.dot(attended, weight_rows, preferred_element_type=jnp.float32)
    return lax.psum_scatter(projected.astype(jnp.bfloat16), "head", scatter_dimension=1, tiled=True)


def solution(mesh):
    heads = mesh.shape["head"]
    seq = mesh.shape["seq"]
    view = Mesh(mesh.devices.reshape(heads, seq // 2, 2), ("head", "chip", "core"))
    return jax.shard_map(
        local,
        mesh=view,
        in_specs=(P(SEQ, "head"), P(SEQ, "head"), P(SEQ, "head"), P("head", SEQ), P(), P()),
        out_specs=P(SEQ, "head"),
        check_vma=False,
    )
```
